256 devices in a mesh: wide: 32 (over x, z), narrow: 8 (over y, core).
Axes of the slice: x: 4, y: 4, z: 8, core: 2. Of those that a mesh axis runs over, the one named last changes fastest.
Arguments:
- embeddings: bfloat16 [524288, 1024], P(('wide', 'narrow')), may hold values from -6 to 6
- level1_ids: int32 [524288], P(('wide', 'narrow')), may hold values from 0 to 32767, as said below
- block_counts: int32 [8192], P(('wide', 'narrow')), may hold values from 1 to 64, as said below
- level1_old: bfloat16 [32768, 1024], P('wide'), may hold values from -6 to 6
- level2_old: bfloat16 [4096, 1024], P('narrow'), may hold values from -6 to 6
- level2_ids: int32 [32768], P('wide'), may hold values from 0 to 4095
Outputs:
- level1_new: bfloat16 [32768, 1024], P('wide')
- level2_new: bfloat16 [4096, 1024], P('narrow')
- split_weights: float32 [4096], P('narrow')
The draws below stay inside these ranges and needn't reach their ends.
Inputs may be any that keep to these rules, and one draw needn't show every extreme that they name: `level1_ids`: in every device's rows, the slots of block b (slot index divided by 64, modulo 32) name level-1 centroids b * 1024 to (b + 1) * 1024 - 1. `block_counts`: at most 64 live slots a block; every device has a block with exactly 64.
All inputs are finite; a program needn't handle non-finite values.
Results may differ from the reference program's by a relative error of at most 0.013.
Values may be sent and summed in bfloat16 or wider, within the bound.
No kernel may reach another device: no remote copies, remote signals or barrier semaphores. Data moves between devices by JAX's collectives and lax.ppermute only.
A program may use at most 64 MiB of HBM per device.

```python
import jax
import jax.numpy as jnp
from jax import lax

D = 1024
CAP = 64
C1_DEV = 1024
K1 = 32768
K2 = 4096
N_ROWS = 524288
N_WIDE = 32
N_NARROW = 8


def draw_level1_ids(key, part):
    slot = jnp.arange(N_ROWS, dtype=jnp.int32)
    block = slot // CAP % N_WIDE
    first = jax.random.randint(jax.random.fold_in(key, 11), (N_ROWS,), 0, C1_DEV)
    second = jax.random.randint(jax.random.fold_in(key, 12), (N_ROWS,), 0, C1_DEV)
    return (block * C1_DEV + jnp.minimum(first, second)).astype(jnp.int32)


def draw_block_counts(key, part):
    device_count = N_WIDE * N_NARROW
    factor = jax.random.randint(jax.random.fold_in(key, 7), (N_WIDE,), 1, 5)
    base = jax.random.randint(jax.random.fold_in(key, 8), (device_count, N_WIDE), 0, CAP)
    counts = 1 + base * (factor[None, :] + 4) // 8
    chosen = jax.random.randint(jax.random.fold_in(key, 9), (device_count,), 0, N_WIDE)
    column = jnp.arange(N_WIDE, dtype=jnp.int32)
    counts = jnp.where(column[None, :] == chosen[:, None], CAP, counts)
    return counts.reshape(-1).astype(jnp.int32)


def place_ends(values, own_key, least, largest):
    place = [jax.random.randint(jax.random.fold_in(own_key, axis), (), 0, length) for axis, length in enumerate(values.shape)]
    longest = values.shape.index(max(values.shape))
    neighbour = place[:longest] + [(place[longest] + 1) % values.shape[longest]] + place[longest + 1:]
    return values.at[tuple(place)].set(least).at[tuple(neighbour)].set(largest)


def levels(own_key, dims, cuts, least, high):
    def one(dim, parts):
        heights = jax.random.uniform(jax.random.fold_in(jax.random.fold_in(own_key, 6), dim), (parts,), jnp.float32, least / len(cuts), high / len(cuts))
        return jnp.repeat(jnp.exp(heights), dims[dim] // parts).reshape((-1,) + (1,) * (len(dims) - dim - 1))

    factor_of = one(*cuts[0])
    for cut in cuts[1:]:
        factor_of = factor_of * one(*cut)
    return factor_of


def centred(key, extent, deviation, limit, pieces=(), kind=jnp.bfloat16):
    result = deviation * jax.random.normal(key, extent, jnp.float32)
    if pieces:
        result = result * levels(key, extent, pieces, -0.22, 0.18)
    return jnp.clip(result, -limit, limit).astype(kind)


def setup_inputs(seed: int = 0) -> dict:
    arg_keys = jax.random.split(jax.random.key(seed), 7)
    embeddings = centred(arg_keys[0], (N_ROWS, D), 1.0, 6.0, ((0, 256),))
    level1_ids = draw_level1_ids(jax.random.fold_in(arg_keys[6], 71), 0)
    block_counts = draw_block_counts(jax.random.fold_in(arg_keys[6], 71), 0)
    level1_old = centred(arg_keys[3], (K1, D), 1.0, 6.0, ((0, 32),))
    level2_old = centred(arg_keys[4], (K2, D), 1.0, 6.0, ((0, 8),))
    level2_ids = place_ends(jax.random.randint(arg_keys[5], (K1,), 0, K2), jax.random.fold_in(arg_keys[5], 1), 0, K2 - 1).astype(jnp.int32)
    return {"embeddings": embeddings, "level1_ids": level1_ids, "block_counts": block_counts, "level1_old": level1_old, "level2_old": level2_old, "level2_ids": level2_ids}


def reference(embeddings, level1_ids, block_counts, level1_old, level2_old, level2_ids):
    per_device = N_WIDE * CAP
    devices = N_WIDE * N_NARROW
    grouped = embeddings.reshape(devices, per_device, D)
    grouped_ids = level1_ids.reshape(devices, per_device)
    position = jnp.arange(per_device, dtype=jnp.int32) % CAP
    limits = jnp.repeat(block_counts.reshape(devices, N_WIDE), CAP, axis=1)
    live_mask = (position[None, :] < limits).astype(jnp.float32)

    def accumulate(carry, items):
        row_block, id_block, mask_block = items
        values = row_block.astype(jnp.float32) * mask_block[:, None]
        sums_new = carry[0] + jax.ops.segment_sum(values, id_block, num_segments=K1)
        counts_new = carry[1] + jax.ops.segment_sum(mask_block, id_block, num_segments=K1)
        return (sums_new, counts_new), None

    start = (jnp.zeros((K1, D), jnp.float32), jnp.zeros((K1,), jnp.float32))
    (sums1, counts1), _ = lax.scan(accumulate, start, (grouped, grouped_ids, live_mask))
    level1_new = ((4.0 * level1_old.astype(jnp.float32) + sums1) / (4.0 + counts1)[:, None]).astype(jnp.bfloat16)
    level1_exact = lax.optimization_barrier(level1_new).astype(jnp.float32)
    sums2 = jax.ops.segment_sum(level1_exact, level2_ids, num_segments=K2)
    counts2 = jax.ops.segment_sum(jnp.ones((K1,), jnp.float32), level2_ids, num_segments=K2)
    squares2 = jax.ops.segment_sum(jnp.sum(level1_exact * level1_exact, axis=1), level2_ids, num_segments=K2)
    means2 = (4.0 * level2_old.astype(jnp.float32) + sums2) / (4.0 + counts2)[:, None]
    inertia = squares2 - 2.0 * jnp.sum(means2 * sums2, axis=1) + counts2 * jnp.sum(means2 * means2, axis=1)
    split_weights = K2 * inertia / jnp.sum(inertia)
    return level1_new, means2.astype(jnp.bfloat16), split_weights
```

```python
import jax
import jax.numpy as jnp
from jax import lax
from jax.sharding import PartitionSpec as P


def split_whole(values, step):
    high = jnp.floor(values / step)
    return high, values - step * high


def split_float(values, pieces):
    out = []
    rest = values
    for _ in range(pieces):
        piece = rest.astype(jnp.bfloat16)
        out.append(piece)
        rest = rest - piece.astype(jnp.float32)
    return out


def pack_rows(body, extras, groups):
    rows, width = body.shape
    per = rows // groups
    flat_body = body.astype(jnp.bfloat16).reshape(groups, per * width)
    tail = jnp.stack([e.astype(jnp.bfloat16).reshape(groups, per) for e in extras], axis=1).reshape(groups, -1)
    pad = (-tail.shape[1]) % 128
    tail = jnp.pad(tail, ((0, 0), (0, pad)))
    return jnp.concatenate([flat_body, tail], axis=1)


def unpack_rows(packed, per, width, n_extras):
    body = packed[:, : per * width].reshape(-1, per, width)
    tail = packed[:, per * width : per * width + n_extras * per].reshape(-1, n_extras, per)
    return body, tail


def local(embeddings, level1_ids, block_counts, level1_old, level2_old, level2_ids):
    wide_count = lax.axis_size("wide")
    narrow_count = lax.axis_size("narrow")
    wide_index = lax.axis_index("wide")
    narrow_index = lax.axis_index("narrow")
    slot_count = embeddings.shape[0] // wide_count
    feature_dim = embeddings.shape[1]
    owner_size = level1_old.shape[0]
    owner_base = wide_index * owner_size
    block_rows = embeddings.reshape(wide_count, slot_count, feature_dim)
    position = lax.broadcasted_iota(jnp.int32, (wide_count, slot_count), 1)
    live_slots = position < block_counts[:, None]
    sent_ids = jnp.where(live_slots, level1_ids.reshape(wide_count, slot_count), -1)
    got_rows = lax.all_to_all(block_rows, "wide", split_axis=0, concat_axis=0, tiled=True)
    got_ids = lax.all_to_all(sent_ids, "wide", split_axis=0, concat_axis=0, tiled=True)

    owner_index = got_ids.reshape(-1) - owner_base
    owner_table = lax.broadcasted_iota(jnp.int32, (owner_size, 1), 0) == owner_index[None, :]
    row_sums = jnp.dot(
        owner_table.astype(jnp.bfloat16),
        got_rows.reshape(-1, feature_dim),
        preferred_element_type=jnp.float32,
    )
    row_counts = jnp.sum(owner_table.astype(jnp.float32), axis=1)

    sub_size = owner_size // narrow_count
    count_high, count_low = split_whole(row_counts, 16.0)
    sent_one = pack_rows(row_sums, [count_high, count_low], narrow_count)
    got_one = lax.all_to_all(sent_one, "narrow", split_axis=0, concat_axis=0, tiled=True)
    body_one, tail_one = unpack_rows(got_one, sub_size, feature_dim, 2)
    sub_sums = jnp.sum(body_one.astype(jnp.float32), axis=0)
    tail_sum = jnp.sum(tail_one.astype(jnp.float32), axis=0)
    sub_counts = 16.0 * tail_sum[0] + tail_sum[1]
    sub_old = lax.dynamic_slice_in_dim(level1_old, narrow_index * sub_size, sub_size, axis=0)
    sub_new = ((4.0 * sub_old.astype(jnp.float32) + sub_sums) / (4.0 + sub_counts)[:, None]).astype(jnp.bfloat16)
    sent_sub = jnp.broadcast_to(sub_new[None], (narrow_count,) + sub_new.shape)
    level1_new = lax.all_to_all(sent_sub, "narrow", split_axis=0, concat_axis=0, tiled=True).reshape(owner_size, feature_dim)

    group_size = level2_old.shape[0]
    group_index = level2_ids - narrow_index * group_size
    group_table = lax.broadcasted_iota(jnp.int32, (group_size, 1), 0) == group_index[None, :]
    group_sums = jnp.dot(group_table.astype(jnp.bfloat16), level1_new, preferred_element_type=jnp.float32)
    group_float = group_table.astype(jnp.float32)
    group_counts = jnp.sum(group_float, axis=1)
    level1_float = level1_new.astype(jnp.float32)
    squares = jnp.sum(level1_float * level1_float, axis=1)
    group_squares = jnp.sum(jnp.where(group_table, squares[None, :], 0.0), axis=1)

    part_size = group_size // wide_count
    squares_high, squares_low = split_float(group_squares, 2)
    counts_high, counts_low = split_whole(group_counts, 16.0)
    sent_two = pack_rows(group_sums, [squares_high, squares_low, counts_high, counts_low], wide_count)
    got_two = lax.all_to_all(sent_two, "wide", split_axis=0, concat_axis=0, tiled=True)
    body_two, tail_two = unpack_rows(got_two, part_size, feature_dim, 4)
    sums_two = jnp.sum(body_two.astype(jnp.float32), axis=0)
    tail_two = jnp.sum(tail_two.astype(jnp.float32), axis=0)
    squares_two = tail_two[0] + tail_two[1]
    counts_two = 16.0 * tail_two[2] + tail_two[3]
    old_two = lax.dynamic_slice_in_dim(level2_old, wide_index * part_size, part_size, axis=0)
    means_two = (4.0 * old_two.astype(jnp.float32) + sums_two) / (4.0 + counts_two)[:, None]
    inertia = (
        squares_two
        - 2.0 * jnp.sum(means_two * sums_two, axis=1)
        + counts_two * jnp.sum(means_two * means_two, axis=1)
    )

    inertia_pieces = split_float(inertia, 3)
    sent_three = pack_rows(means_two, inertia_pieces, 1)
    sent_three = jnp.broadcast_to(sent_three, (wide_count, sent_three.shape[1]))
    got_three = lax.all_to_all(sent_three, "wide", split_axis=0, concat_axis=0, tiled=True)
    body_three, tail_three = unpack_rows(got_three, part_size, feature_dim, 3)
    level2_new = body_three.reshape(group_size, feature_dim)
    tail_three = tail_three.astype(jnp.float32)
    inertia_all = ((tail_three[:, 0] + tail_three[:, 1]) + tail_three[:, 2]).reshape(group_size)
    inertia_sum = lax.psum(jnp.sum(inertia_all), "narrow")
    centroid_total = float(group_size * narrow_count)
    split_weights = centroid_total * inertia_all / inertia_sum
    return (level1_new, level2_new, split_weights)


def solution(mesh):
    return jax.shard_map(
        local,
        mesh=mesh,
        in_specs=(
            P(("wide", "narrow"), None),
            P(("wide", "narrow")),
            P(("wide", "narrow")),
            P("wide", None),
            P("narrow", None),
            P("wide"),
        ),
        out_specs=(P("wide", None), P("narrow", None), P("narrow")),
        check_vma=False,
    )
```

```python
import jax
import jax.numpy as jnp
from jax import lax
from jax.sharding import PartitionSpec as P


def split_whole(values, step):
    high = jnp.floor(values / step)
    return high, values - step * high


def split_float(values, pieces):
    out = []
    rest = values
    for _ in range(pieces):
        piece = rest.astype(jnp.bfloat16)
        out.append(piece)
        rest = rest - piece.astype(jnp.float32)
    return out


def pack_columns(body, extras):
    rows = body.shape[0]
    lane = lax.broadcasted_iota(jnp.int32, (rows, 128), 1)
    tail = jnp.zeros((rows, 128), jnp.float32)
    for place, extra in enumerate(extras):
        tail = jnp.where(lane == place, extra.astype(jnp.float32)[:, None], tail)
    return jnp.concatenate([body.astype(jnp.bfloat16), tail.astype(jnp.bfloat16)], axis=1)


def local(embeddings, level1_ids, block_counts, level1_old, level2_old, level2_ids):
    wide_count = lax.axis_size("wide")
    narrow_count = lax.axis_size("narrow")
    wide_index = lax.axis_index("wide")
    narrow_index = lax.axis_index("narrow")
    slot_count = embeddings.shape[0] // wide_count
    feature_dim = embeddings.shape[1]
    owner_size = level1_old.shape[0]
    owner_base = wide_index * owner_size
    block_rows = embeddings.reshape(wide_count, slot_count, feature_dim)
    position = lax.broadcasted_iota(jnp.int32, (wide_count, slot_count), 1)
    live_slots = position < block_counts[:, None]
    sent_ids = jnp.where(live_slots, level1_ids.reshape(wide_count, slot_count), -1)
    got_rows = lax.all_to_all(block_rows, "wide", split_axis=0, concat_axis=0, tiled=True)
    got_ids = lax.all_to_all(sent_ids, "wide", split_axis=0, concat_axis=0, tiled=True)

    owner_index = got_ids.reshape(-1) - owner_base
    owner_table = lax.broadcasted_iota(jnp.int32, (owner_size, 1), 0) == owner_index[None, :]
    row_sums = jnp.dot(
        owner_table.astype(jnp.bfloat16),
        got_rows.reshape(-1, feature_dim),
        preferred_element_type=jnp.float32,
    )
    row_counts = jnp.dot(
        owner_table.astype(jnp.bfloat16),
        jnp.ones((owner_index.shape[0], 128), jnp.bfloat16),
        preferred_element_type=jnp.float32,
    )[:, 0]

    sub_size = owner_size // narrow_count
    count_high, count_low = split_whole(row_counts, 16.0)
    sent_one = pack_columns(row_sums, [count_high, count_low]).reshape(narrow_count, sub_size, -1)
    got_one = lax.all_to_all(sent_one, "narrow", split_axis=0, concat_axis=0, tiled=True)
    sub_sums = jnp.sum(got_one[:, :, :feature_dim].astype(jnp.float32), axis=0)
    tail_sum = jnp.sum(got_one[:, :, feature_dim : feature_dim + 2].astype(jnp.float32), axis=0)
    sub_counts = 16.0 * tail_sum[:, 0] + tail_sum[:, 1]
    sub_old = lax.dynamic_slice_in_dim(level1_old, narrow_index * sub_size, sub_size, axis=0)
    sub_new = ((4.0 * sub_old.astype(jnp.float32) + sub_sums) / (4.0 + sub_counts)[:, None]).astype(jnp.bfloat16)
    sent_sub = jnp.broadcast_to(sub_new[None], (narrow_count,) + sub_new.shape)
    level1_new = lax.all_to_all(sent_sub, "narrow", split_axis=0, concat_axis=0, tiled=True).reshape(owner_size, feature_dim)

    group_size = level2_old.shape[0]
    group_index = level2_ids - narrow_index * group_size
    group_table = lax.broadcasted_iota(jnp.int32, (group_size, 1), 0) == group_index[None, :]
    group_sums = jnp.dot(group_table.astype(jnp.bfloat16), level1_new, preferred_element_type=jnp.float32)
    group_counts = jnp.dot(
        group_table.astype(jnp.bfloat16),
        jnp.ones((group_index.shape[0], 128), jnp.bfloat16),
        preferred_element_type=jnp.float32,
    )[:, 0]
    level1_float = level1_new.astype(jnp.float32)
    squares = jnp.sum(level1_float * level1_float, axis=1)
    group_squares = jnp.sum(jnp.where(group_table, squares[None, :], 0.0), axis=1)

    part_size = group_size // wide_count
    squares_high, squares_low = split_float(group_squares, 2)
    counts_high, counts_low = split_whole(group_counts, 16.0)
    sent_two = pack_columns(group_sums, [squares_high, squares_low, counts_high, counts_low])
    sent_two = sent_two.reshape(wide_count, part_size, -1)
    got_two = lax.all_to_all(sent_two, "wide", split_axis=0, concat_axis=0, tiled=True)
    sums_two = jnp.sum(got_two[:, :, :feature_dim].astype(jnp.float32), axis=0)
    tail_two = jnp.sum(got_two[:, :, feature_dim : feature_dim + 4].astype(jnp.float32), axis=0)
    squares_two = tail_two[:, 0] + tail_two[:, 1]
    counts_two = 16.0 * tail_two[:, 2] + tail_two[:, 3]
    old_two = lax.dynamic_slice_in_dim(level2_old, wide_index * part_size, part_size, axis=0)
    means_two = (4.0 * old_two.astype(jnp.float32) + sums_two) / (4.0 + counts_two)[:, None]
    inertia = (
        squares_two
        - 2.0 * jnp.sum(means_two * sums_two, axis=1)
        + counts_two * jnp.sum(means_two * means_two, axis=1)
    )

    inertia_pieces = split_float(inertia, 3)
    sent_three = pack_columns(means_two, inertia_pieces)
    sent_three = jnp.broadcast_to(sent_three[None], (wide_count,) + sent_three.shape)
    got_three = lax.all_to_all(sent_three, "wide", split_axis=0, concat_axis=0, tiled=True)
    level2_new = got_three[:, :, :feature_dim].reshape(group_size, feature_dim)
    tail_three = got_three[:, :, feature_dim : feature_dim + 3].astype(jnp.float32)
    inertia_all = ((tail_three[:, :, 0] + tail_three[:, :, 1]) + tail_three[:, :, 2]).reshape(group_size)
    inertia_sum = lax.psum(jnp.sum(inertia_all), "narrow")
    centroid_total = float(group_size * narrow_count)
    split_weights = centroid_total * inertia_all / inertia_sum
    return (level1_new, level2_new, split_weights)


def solution(mesh):
    return jax.shard_map(
        local,
        mesh=mesh,
        in_specs=(
            P(("wide", "narrow"), None),
            P(("wide", "narrow")),
            P(("wide", "narrow")),
            P("wide", None),
            P("narrow", None),
            P("wide"),
        ),
        out_specs=(P("wide", None), P("narrow", None), P("narrow")),
        check_vma=False,
    )
```

```python
import jax
import jax.numpy as jnp
from jax import lax
from jax.sharding import PartitionSpec as P


def split_whole(values, step):
    high = jnp.floor(values / step)
    return high, values - step * high


def split_float(values, pieces):
    out = []
    rest = values
    for _ in range(pieces):
        piece = rest.astype(jnp.bfloat16)
        out.append(piece)
        rest = rest - piece.astype(jnp.float32)
    return out


def pack_columns(body, extras):
    rows = body.shape[0]
    lane = lax.broadcasted_iota(jnp.int32, (rows, 128), 1)
    tail = jnp.zeros((rows, 128), jnp.float32)
    for place, extra in enumerate(extras):
        tail = jnp.where(lane == place, extra.astype(jnp.float32)[:, None], tail)
    return jnp.concatenate([body.astype(jnp.bfloat16), tail.astype(jnp.bfloat16)], axis=1)


def local(embeddings, level1_ids, block_counts, level1_old, level2_old, level2_ids):
    wide_count = lax.axis_size("wide")
    narrow_count = lax.axis_size("narrow")
    wide_index = lax.axis_index("wide")
    narrow_index = lax.axis_index("narrow")
    slot_count = embeddings.shape[0] // wide_count
    feature_dim = embeddings.shape[1]
    owner_size = level1_old.shape[0]
    owner_base = wide_index * owner_size
    block_rows = embeddings.reshape(wide_count, slot_count, feature_dim)
    position = lax.broadcasted_iota(jnp.int32, (wide_count, slot_count), 1)
    live_slots = position < block_counts[:, None]
    lanes = 128
    pieces = feature_dim // lanes
    block_base = lax.broadcasted_iota(jnp.int32, (wide_count, 1), 0) * owner_size
    local_ids = jnp.where(live_slots, level1_ids.reshape(wide_count, slot_count) - block_base, -32)
    id_high = jnp.floor_divide(local_ids, 32)
    id_low = local_ids - 32 * id_high
    id_flat = jnp.concatenate([id_high, id_low], axis=1).astype(jnp.float32).astype(jnp.bfloat16)
    tile_rows = -(-id_flat.shape[1] // lanes)
    tile_pad = -(-tile_rows // 16) * 16
    id_flat = jnp.pad(id_flat, ((0, 0), (0, tile_pad * lanes - id_flat.shape[1])))
    id_tile = id_flat.reshape(wide_count, tile_pad, lanes)
    body_rows = block_rows.reshape(wide_count, slot_count * pieces, lanes)
    sent_rows = jnp.concatenate([body_rows, id_tile], axis=1)
    got_all = lax.all_to_all(sent_rows, "wide", split_axis=0, concat_axis=0, tiled=True)
    got_rows = got_all[:, : slot_count * pieces, :].reshape(wide_count * slot_count, feature_dim)
    got_tile = got_all[:, slot_count * pieces :, :].reshape(wide_count, -1)[:, : 2 * slot_count].astype(jnp.float32)
    got_local = (32.0 * got_tile[:, :slot_count] + got_tile[:, slot_count:]).astype(jnp.int32)

    owner_index = got_local.reshape(-1)
    owner_table = lax.broadcasted_iota(jnp.int32, (owner_size, 1), 0) == owner_index[None, :]
    row_sums = jnp.dot(
        owner_table.astype(jnp.bfloat16),
        got_rows,
        preferred_element_type=jnp.float32,
    )
    row_counts = jnp.dot(
        owner_table.astype(jnp.bfloat16),
        jnp.ones((owner_index.shape[0], 128), jnp.bfloat16),
        preferred_element_type=jnp.float32,
    )[:, 0]

    sub_size = owner_size // narrow_count
    count_high, count_low = split_whole(row_counts, 16.0)
    sent_one = pack_columns(row_sums, [count_high, count_low]).reshape(narrow_count, sub_size, -1)
    got_one = lax.all_to_all(sent_one, "narrow", split_axis=0, concat_axis=0, tiled=True)
    sub_sums = jnp.sum(got_one[:, :, :feature_dim].astype(jnp.float32), axis=0)
    tail_sum = jnp.sum(got_one[:, :, feature_dim : feature_dim + 2].astype(jnp.float32), axis=0)
    sub_counts = 16.0 * tail_sum[:, 0] + tail_sum[:, 1]
    sub_old = lax.dynamic_slice_in_dim(level1_old, narrow_index * sub_size, sub_size, axis=0)
    sub_new = ((4.0 * sub_old.astype(jnp.float32) + sub_sums) / (4.0 + sub_counts)[:, None]).astype(jnp.bfloat16)
    sent_sub = jnp.broadcast_to(sub_new[None], (narrow_count,) + sub_new.shape)
    level1_new = lax.all_to_all(sent_sub, "narrow", split_axis=0, concat_axis=0, tiled=True).reshape(owner_size, feature_dim)

    group_size = level2_old.shape[0]
    group_index = level2_ids - narrow_index * group_size
    group_table = lax.broadcasted_iota(jnp.int32, (group_size, 1), 0) == group_index[None, :]
    group_sums = jnp.dot(group_table.astype(jnp.bfloat16), level1_new, preferred_element_type=jnp.float32)
    group_counts = jnp.dot(
        group_table.astype(jnp.bfloat16),
        jnp.ones((group_index.shape[0], 128), jnp.bfloat16),
        preferred_element_type=jnp.float32,
    )[:, 0]
    level1_float = level1_new.astype(jnp.float32)
    squares = jnp.sum(level1_float * level1_float, axis=1)
    group_squares = jnp.sum(jnp.where(group_table, squares[None, :], 0.0), axis=1)

    part_size = group_size // wide_count
    squares_high, squares_low = split_float(group_squares, 2)
    counts_high, counts_low = split_whole(group_counts, 16.0)
    sent_two = pack_columns(group_sums, [squares_high, squares_low, counts_high, counts_low])
    sent_two = sent_two.reshape(wide_count, part_size, -1)
    got_two = lax.all_to_all(sent_two, "wide", split_axis=0, concat_axis=0, tiled=True)
    sums_two = jnp.sum(got_two[:, :, :feature_dim].astype(jnp.float32), axis=0)
    tail_two = jnp.sum(got_two[:, :, feature_dim : feature_dim + 4].astype(jnp.float32), axis=0)
    squares_two = tail_two[:, 0] + tail_two[:, 1]
    counts_two = 16.0 * tail_two[:, 2] + tail_two[:, 3]
    old_two = lax.dynamic_slice_in_dim(level2_old, wide_index * part_size, part_size, axis=0)
    means_two = (4.0 * old_two.astype(jnp.float32) + sums_two) / (4.0 + counts_two)[:, None]
    inertia = (
        squares_two
        - 2.0 * jnp.sum(means_two * sums_two, axis=1)
        + counts_two * jnp.sum(means_two * means_two, axis=1)
    )

    inertia_pieces = split_float(inertia, 3)
    sent_three = pack_columns(means_two, inertia_pieces)
    sent_three = jnp.broadcast_to(sent_three[None], (wide_count,) + sent_three.shape)
    got_three = lax.all_to_all(sent_three, "wide", split_axis=0, concat_axis=0, tiled=True)
    level2_new = got_three[:, :, :feature_dim].reshape(group_size, feature_dim)
    tail_three = got_three[:, :, feature_dim : feature_dim + 3].astype(jnp.float32)
    inertia_all = ((tail_three[:, :, 0] + tail_three[:, :, 1]) + tail_three[:, :, 2]).reshape(group_size)
    inertia_sum = lax.psum(jnp.sum(inertia_all), "narrow")
    centroid_total = float(group_size * narrow_count)
    split_weights = centroid_total * inertia_all / inertia_sum
    return (level1_new, level2_new, split_weights)


def solution(mesh):
    return jax.shard_map(
        local,
        mesh=mesh,
        in_specs=(
            P(("wide", "narrow"), None),
            P(("wide", "narrow")),
            P(("wide", "narrow")),
            P("wide", None),
            P("narrow", None),
            P("wide"),
        ),
        out_specs=(P("wide", None), P("narrow", None), P("narrow")),
        check_vma=False,
    )
```

```python
import jax
import jax.numpy as jnp
from jax import lax
from jax.sharding import PartitionSpec as P


def split_whole(values, step):
    high = jnp.floor(values / step)
    return high, values - step * high


def split_float(values, pieces):
    out = []
    rest = values
    for _ in range(pieces):
        piece = rest.astype(jnp.bfloat16)
        out.append(piece)
        rest = rest - piece.astype(jnp.float32)
    return out


def pack_columns(body, extras):
    rows = body.shape[0]
    lane = lax.broadcasted_iota(jnp.int32, (rows, 128), 1)
    tail = jnp.zeros((rows, 128), jnp.float32)
    for place, extra in enumerate(extras):
        tail = jnp.where(lane == place, extra.astype(jnp.float32)[:, None], tail)
    return jnp.concatenate([body.astype(jnp.bfloat16), tail.astype(jnp.bfloat16)], axis=1)


def local(embeddings, level1_ids, block_counts, level1_old, level2_old, level2_ids):
    wide_count = lax.axis_size("wide")
    narrow_count = lax.axis_size("narrow")
    wide_index = lax.axis_index("wide")
    narrow_index = lax.axis_index("narrow")
    slot_count = embeddings.shape[0] // wide_count
    feature_dim = embeddings.shape[1]
    owner_size = level1_old.shape[0]
    owner_base = wide_index * owner_size
    block_rows = embeddings.reshape(wide_count, slot_count, feature_dim)
    position = lax.broadcasted_iota(jnp.int32, (wide_count, slot_count), 1)
    live_slots = position < block_counts[:, None]
    sent_ids = jnp.where(live_slots, level1_ids.reshape(wide_count, slot_count), -1)
    got_rows = lax.all_to_all(block_rows, "wide", split_axis=0, concat_axis=0, tiled=True)
    got_ids = lax.all_to_all(sent_ids, "wide", split_axis=0, concat_axis=0, tiled=True)

    owner_index = got_ids.reshape(-1) - owner_base
    owner_table = lax.broadcasted_iota(jnp.int32, (owner_size, 1), 0) == owner_index[None, :]
    row_sums = jnp.dot(
        owner_table.astype(jnp.bfloat16),
        got_rows.reshape(-1, feature_dim),
        preferred_element_type=jnp.float32,
    )
    row_counts = jnp.dot(
        owner_table.astype(jnp.bfloat16),
        jnp.ones((owner_index.shape[0], 128), jnp.bfloat16),
        preferred_element_type=jnp.float32,
    )[:, 0]

    core_count = 2
    chip_count = narrow_count // core_count
    core = narrow_index % core_count
    chip = narrow_index // core_count
    half_size = owner_size // core_count
    sub_size = half_size // chip_count
    count_high, count_low = split_whole(row_counts, 16.0)
    packed = pack_columns(row_sums, [count_high, count_low]).reshape(core_count, half_size, -1)
    kept = jnp.where(core == 0, packed[0], packed[1])
    given = jnp.where(core == 0, packed[1], packed[0])
    partner = [(i, i ^ 1) for i in range(narrow_count)]
    chip_part = kept.astype(jnp.float32) + lax.ppermute(given, "narrow", partner).astype(jnp.float32)
    rings = [[c + core_count * y for y in range(chip_count)] for c in range(core_count)]
    sent_one = chip_part.astype(jnp.bfloat16).reshape(chip_count, sub_size, -1)
    got_one = lax.all_to_all(sent_one, "narrow", 0, 0, axis_index_groups=rings, tiled=True)
    sub_sums = jnp.sum(got_one[:, :, :feature_dim].astype(jnp.float32), axis=0)
    tail_sum = jnp.sum(got_one[:, :, feature_dim : feature_dim + 2].astype(jnp.float32), axis=0)
    sub_counts = 16.0 * tail_sum[:, 0] + tail_sum[:, 1]
    sub_start = core * half_size + chip * sub_size
    sub_old = lax.dynamic_slice_in_dim(level1_old, sub_start, sub_size, axis=0)
    sub_new = ((4.0 * sub_old.astype(jnp.float32) + sub_sums) / (4.0 + sub_counts)[:, None]).astype(jnp.bfloat16)
    sent_sub = jnp.broadcast_to(sub_new[None], (chip_count,) + sub_new.shape)
    half_new = lax.all_to_all(sent_sub, "narrow", 0, 0, axis_index_groups=rings, tiled=True).reshape(half_size, feature_dim)
    other_half = lax.ppermute(half_new, "narrow", partner)
    level1_new = jnp.where(
        core == 0,
        jnp.concatenate([half_new, other_half], axis=0),
        jnp.concatenate([other_half, half_new], axis=0),
    )

    group_size = level2_old.shape[0]
    group_index = level2_ids - narrow_index * group_size
    group_table = lax.broadcasted_iota(jnp.int32, (group_size, 1), 0) == group_index[None, :]
    group_sums = jnp.dot(group_table.astype(jnp.bfloat16), level1_new, preferred_element_type=jnp.float32)
    group_counts = jnp.dot(
        group_table.astype(jnp.bfloat16),
        jnp.ones((group_index.shape[0], 128), jnp.bfloat16),
        preferred_element_type=jnp.float32,
    )[:, 0]
    level1_float = level1_new.astype(jnp.float32)
    squares = jnp.sum(level1_float * level1_float, axis=1)
    group_squares = jnp.sum(jnp.where(group_table, squares[None, :], 0.0), axis=1)

    part_size = group_size // wide_count
    squares_high, squares_low = split_float(group_squares, 2)
    counts_high, counts_low = split_whole(group_counts, 16.0)
    sent_two = pack_columns(group_sums, [squares_high, squares_low, counts_high, counts_low])
    sent_two = sent_two.reshape(wide_count, part_size, -1)
    got_two = lax.all_to_all(sent_two, "wide", split_axis=0, concat_axis=0, tiled=True)
    sums_two = jnp.sum(got_two[:, :, :feature_dim].astype(jnp.float32), axis=0)
    tail_two = jnp.sum(got_two[:, :, feature_dim : feature_dim + 4].astype(jnp.float32), axis=0)
    squares_two = tail_two[:, 0] + tail_two[:, 1]
    counts_two = 16.0 * tail_two[:, 2] + tail_two[:, 3]
    old_two = lax.dynamic_slice_in_dim(level2_old, wide_index * part_size, part_size, axis=0)
    means_two = (4.0 * old_two.astype(jnp.float32) + sums_two) / (4.0 + counts_two)[:, None]
    inertia = (
        squares_two
        - 2.0 * jnp.sum(means_two * sums_two, axis=1)
        + counts_two * jnp.sum(means_two * means_two, axis=1)
    )

    inertia_pieces = split_float(inertia, 3)
    sent_three = pack_columns(means_two, inertia_pieces)
    sent_three = jnp.broadcast_to(sent_three[None], (wide_count,) + sent_three.shape)
    got_three = lax.all_to_all(sent_three, "wide", split_axis=0, concat_axis=0, tiled=True)
    level2_new = got_three[:, :, :feature_dim].reshape(group_size, feature_dim)
    tail_three = got_three[:, :, feature_dim : feature_dim + 3].astype(jnp.float32)
    inertia_all = ((tail_three[:, :, 0] + tail_three[:, :, 1]) + tail_three[:, :, 2]).reshape(group_size)
    inertia_sum = lax.psum(jnp.sum(inertia_all), "narrow")
    centroid_total = float(group_size * narrow_count)
    split_weights = centroid_total * inertia_all / inertia_sum
    return (level1_new, level2_new, split_weights)


def solution(mesh):
    return jax.shard_map(
        local,
        mesh=mesh,
        in_specs=(
            P(("wide", "narrow"), None),
            P(("wide", "narrow")),
            P(("wide", "narrow")),
            P("wide", None),
            P("narrow", None),
            P("wide"),
        ),
        out_specs=(P("wide", None), P("narrow", None), P("narrow")),
        check_vma=False,
    )
```

```python
import jax
import jax.numpy as jnp
from jax import lax
from jax.sharding import PartitionSpec as P


def split_whole(values, step):
    high = jnp.floor(values / step)
    return high, values - step * high


def split_float(values, pieces):
    out = []
    rest = values
    for _ in range(pieces):
        piece = rest.astype(jnp.bfloat16)
        out.append(piece)
        rest = rest - piece.astype(jnp.float32)
    return out


def pack_columns(body, extras):
    rows = body.shape[0]
    lane = lax.broadcasted_iota(jnp.int32, (rows, 128), 1)
    tail = jnp.zeros((rows, 128), jnp.float32)
    for place, extra in enumerate(extras):
        tail = jnp.where(lane == place, extra.astype(jnp.float32)[:, None], tail)
    return jnp.concatenate([body.astype(jnp.bfloat16), tail.astype(jnp.bfloat16)], axis=1)


def local(embeddings, level1_ids, block_counts, level1_old, level2_old, level2_ids):
    wide_count = lax.axis_size("wide")
    narrow_count = lax.axis_size("narrow")
    wide_index = lax.axis_index("wide")
    narrow_index = lax.axis_index("narrow")
    slot_count = embeddings.shape[0] // wide_count
    feature_dim = embeddings.shape[1]
    owner_size = level1_old.shape[0]
    owner_base = wide_index * owner_size
    block_rows = embeddings.reshape(wide_count, slot_count, feature_dim)
    position = lax.broadcasted_iota(jnp.int32, (wide_count, slot_count), 1)
    live_slots = position < block_counts[:, None]
    sent_ids = jnp.where(live_slots, level1_ids.reshape(wide_count, slot_count), -1)
    got_rows = lax.all_to_all(block_rows, "wide", split_axis=0, concat_axis=0, tiled=True)
    got_ids = lax.all_to_all(sent_ids, "wide", split_axis=0, concat_axis=0, tiled=True)

    owner_index = got_ids.reshape(-1) - owner_base
    owner_table = lax.broadcasted_iota(jnp.int32, (owner_size, 1), 0) == owner_index[None, :]
    row_sums = jnp.dot(
        owner_table.astype(jnp.bfloat16),
        got_rows.reshape(-1, feature_dim),
        preferred_element_type=jnp.float32,
    )
    row_counts = jnp.dot(
        owner_table.astype(jnp.bfloat16),
        jnp.ones((owner_index.shape[0], 128), jnp.bfloat16),
        preferred_element_type=jnp.float32,
    )[:, 0]

    core_count = 2
    chip_count = narrow_count // core_count
    core = narrow_index % core_count
    chip = narrow_index // core_count
    half_size = owner_size // core_count
    sub_size = half_size // chip_count
    count_high, count_low = split_whole(row_counts, 16.0)
    packed = pack_columns(row_sums, [count_high, count_low]).reshape(core_count, half_size, -1)
    kept = jnp.where(core == 0, packed[0], packed[1])
    given = jnp.where(core == 0, packed[1], packed[0])
    partner = [(i, i ^ 1) for i in range(narrow_count)]
    chip_part = kept.astype(jnp.float32) + lax.ppermute(given, "narrow", partner).astype(jnp.float32)
    rings = [[c + core_count * y for y in range(chip_count)] for c in range(core_count)]
    sent_one = chip_part.astype(jnp.bfloat16).reshape(chip_count, sub_size, -1)
    got_one = lax.all_to_all(sent_one, "narrow", 0, 0, axis_index_groups=rings, tiled=True)
    sub_sums = jnp.sum(got_one[:, :, :feature_dim].astype(jnp.float32), axis=0)
    tail_sum = jnp.sum(got_one[:, :, feature_dim : feature_dim + 2].astype(jnp.float32), axis=0)
    sub_counts = 16.0 * tail_sum[:, 0] + tail_sum[:, 1]
    sub_start = core * half_size + chip * sub_size
    sub_old = lax.dynamic_slice_in_dim(level1_old, sub_start, sub_size, axis=0)
    sub_new = ((4.0 * sub_old.astype(jnp.float32) + sub_sums) / (4.0 + sub_counts)[:, None]).astype(jnp.bfloat16)
    sent_sub = jnp.broadcast_to(sub_new[None], (chip_count,) + sub_new.shape)
    half_new = lax.all_to_all(sent_sub, "narrow", 0, 0, axis_index_groups=rings, tiled=True).reshape(half_size, feature_dim)
    other_half = lax.ppermute(half_new, "narrow", partner)
    level1_new = jnp.where(
        core == 0,
        jnp.concatenate([half_new, other_half], axis=0),
        jnp.concatenate([other_half, half_new], axis=0),
    )

    group_size = level2_old.shape[0]
    group_index = level2_ids - narrow_index * group_size
    group_table = lax.broadcasted_iota(jnp.int32, (group_size, 1), 0) == group_index[None, :]
    group_sums = jnp.dot(group_table.astype(jnp.bfloat16), level1_new, preferred_element_type=jnp.float32)
    group_counts = jnp.dot(
        group_table.astype(jnp.bfloat16),
        jnp.ones((group_index.shape[0], 128), jnp.bfloat16),
        preferred_element_type=jnp.float32,
    )[:, 0]
    level1_float = level1_new.astype(jnp.float32)
    squares = jnp.sum(level1_float * level1_float, axis=1)
    group_squares = jnp.sum(jnp.where(group_table, squares[None, :], 0.0), axis=1)

    part_size = group_size // wide_count
    z_count = 8
    x_count = wide_count // z_count
    x_rings = [[z + z_count * x for x in range(x_count)] for z in range(z_count)]
    z_rings = [[z + z_count * x for z in range(z_count)] for x in range(x_count)]
    squares_high, squares_low = split_float(group_squares, 2)
    counts_high, counts_low = split_whole(group_counts, 16.0)
    sent_two = pack_columns(group_sums, [squares_high, squares_low, counts_high, counts_low])
    sent_two = sent_two.reshape(x_count, z_count * part_size, -1)
    got_x = lax.all_to_all(sent_two, "wide", 0, 0, axis_index_groups=x_rings, tiled=True)
    x_sums = jnp.sum(got_x[:, :, :feature_dim].astype(jnp.float32), axis=0)
    x_tail = jnp.sum(got_x[:, :, feature_dim : feature_dim + 4].astype(jnp.float32), axis=0)
    x_squares = x_tail[:, 0] + x_tail[:, 1]
    x_counts = 16.0 * x_tail[:, 2] + x_tail[:, 3]
    squares_high, squares_low = split_float(x_squares, 2)
    counts_high, counts_low = split_whole(x_counts, 16.0)
    sent_z = pack_columns(x_sums, [squares_high, squares_low, counts_high, counts_low])
    sent_z = sent_z.reshape(z_count, part_size, -1)
    got_two = lax.all_to_all(sent_z, "wide", 0, 0, axis_index_groups=z_rings, tiled=True)
    sums_two = jnp.sum(got_two[:, :, :feature_dim].astype(jnp.float32), axis=0)
    tail_two = jnp.sum(got_two[:, :, feature_dim : feature_dim + 4].astype(jnp.float32), axis=0)
    squares_two = tail_two[:, 0] + tail_two[:, 1]
    counts_two = 16.0 * tail_two[:, 2] + tail_two[:, 3]
    old_two = lax.dynamic_slice_in_dim(level2_old, wide_index * part_size, part_size, axis=0)
    means_two = (4.0 * old_two.astype(jnp.float32) + sums_two) / (4.0 + counts_two)[:, None]
    inertia = (
        squares_two
        - 2.0 * jnp.sum(means_two * sums_two, axis=1)
        + counts_two * jnp.sum(means_two * means_two, axis=1)
    )

    inertia_pieces = split_float(inertia, 3)
    sent_three = pack_columns(means_two, inertia_pieces)
    sent_three = jnp.broadcast_to(sent_three[None], (z_count,) + sent_three.shape)
    got_z = lax.all_to_all(sent_three, "wide", 0, 0, axis_index_groups=z_rings, tiled=True)
    sent_x = jnp.broadcast_to(got_z[None], (x_count,) + got_z.shape)
    got_three = lax.all_to_all(sent_x, "wide", 0, 0, axis_index_groups=x_rings, tiled=True)
    got_three = got_three.reshape(wide_count, part_size, -1)
    level2_new = got_three[:, :, :feature_dim].reshape(group_size, feature_dim)
    tail_three = got_three[:, :, feature_dim : feature_dim + 3].astype(jnp.float32)
    inertia_all = ((tail_three[:, :, 0] + tail_three[:, :, 1]) + tail_three[:, :, 2]).reshape(group_size)
    inertia_sum = lax.psum(jnp.sum(inertia_all), "narrow")
    centroid_total = float(group_size * narrow_count)
    split_weights = centroid_total * inertia_all / inertia_sum
    return (level1_new, level2_new, split_weights)


def solution(mesh):
    return jax.shard_map(
        local,
        mesh=mesh,
        in_specs=(
            P(("wide", "narrow"), None),
            P(("wide", "narrow")),
            P(("wide", "narrow")),
            P("wide", None),
            P("narrow", None),
            P("wide"),
        ),
        out_specs=(P("wide", None), P("narrow", None), P("narrow")),
        check_vma=False,
    )
```

```python
import jax
import jax.numpy as jnp
from jax import lax
from jax.sharding import PartitionSpec as P


def split_whole(values, step):
    high = jnp.floor(values / step)
    return high, values - step * high


def split_float(values, pieces):
    out = []
    rest = values
    for _ in range(pieces):
        piece = rest.astype(jnp.bfloat16)
        out.append(piece)
        rest = rest - piece.astype(jnp.float32)
    return out


def pack_columns(body, extras):
    rows = body.shape[0]
    lane = lax.broadcasted_iota(jnp.int32, (rows, 128), 1)
    tail = jnp.zeros((rows, 128), jnp.float32)
    for place, extra in enumerate(extras):
        tail = jnp.where(lane == place, extra.astype(jnp.float32)[:, None], tail)
    return jnp.concatenate([body.astype(jnp.bfloat16), tail.astype(jnp.bfloat16)], axis=1)


def local(embeddings, level1_ids, block_counts, level1_old, level2_old, level2_ids):
    wide_count = lax.axis_size("wide")
    narrow_count = lax.axis_size("narrow")
    wide_index = lax.axis_index("wide")
    narrow_index = lax.axis_index("narrow")
    slot_count = embeddings.shape[0] // wide_count
    feature_dim = embeddings.shape[1]
    owner_size = level1_old.shape[0]
    owner_base = wide_index * owner_size
    block_rows = embeddings.reshape(wide_count, slot_count, feature_dim)
    position = lax.broadcasted_iota(jnp.int32, (wide_count, slot_count), 1)
    live_slots = position < block_counts[:, None]
    sent_ids = jnp.where(live_slots, level1_ids.reshape(wide_count, slot_count), -1)
    got_rows = lax.all_to_all(block_rows, "wide", split_axis=0, concat_axis=0, tiled=True)
    got_ids = lax.all_to_all(sent_ids, "wide", split_axis=0, concat_axis=0, tiled=True)

    owner_index = got_ids.reshape(-1) - owner_base
    owner_table = lax.broadcasted_iota(jnp.int32, (owner_size, 1), 0) == owner_index[None, :]
    row_sums = jnp.dot(
        owner_table.astype(jnp.bfloat16),
        got_rows.reshape(-1, feature_dim),
        preferred_element_type=jnp.float32,
    )
    row_counts = jnp.dot(
        owner_table.astype(jnp.bfloat16),
        jnp.ones((owner_index.shape[0], 128), jnp.bfloat16),
        preferred_element_type=jnp.float32,
    )[:, 0]

    core_count = 2
    chip_count = narrow_count // core_count
    core = narrow_index % core_count
    chip = narrow_index // core_count
    half_size = owner_size // core_count
    sub_size = half_size // chip_count
    count_high, count_low = split_whole(row_counts, 16.0)
    packed = pack_columns(row_sums, [count_high, count_low]).reshape(core_count, half_size, -1)
    kept = jnp.where(core == 0, packed[0], packed[1])
    given = jnp.where(core == 0, packed[1], packed[0])
    partner = [(i, i ^ 1) for i in range(narrow_count)]
    chip_part = kept.astype(jnp.float32) + lax.ppermute(given, "narrow", partner).astype(jnp.float32)
    rings = [[c + core_count * y for y in range(chip_count)] for c in range(core_count)]
    sent_one = chip_part.astype(jnp.bfloat16).reshape(chip_count, sub_size, -1)
    got_one = lax.all_to_all(sent_one, "narrow", 0, 0, axis_index_groups=rings, tiled=True)
    sub_sums = jnp.sum(got_one[:, :, :feature_dim].astype(jnp.float32), axis=0)
    tail_sum = jnp.sum(got_one[:, :, feature_dim : feature_dim + 2].astype(jnp.float32), axis=0)
    sub_counts = 16.0 * tail_sum[:, 0] + tail_sum[:, 1]
    sub_start = core * half_size + chip * sub_size
    sub_old = lax.dynamic_slice_in_dim(level1_old, sub_start, sub_size, axis=0)
    sub_new = ((4.0 * sub_old.astype(jnp.float32) + sub_sums) / (4.0 + sub_counts)[:, None]).astype(jnp.bfloat16)
    sent_sub = jnp.broadcast_to(sub_new[None], (chip_count,) + sub_new.shape)
    half_new = lax.all_to_all(sent_sub, "narrow", 0, 0, axis_index_groups=rings, tiled=True).reshape(half_size, feature_dim)
    other_half = lax.ppermute(half_new, "narrow", partner)
    level1_new = jnp.where(
        core == 0,
        jnp.concatenate([half_new, other_half], axis=0),
        jnp.concatenate([other_half, half_new], axis=0),
    )

    group_size = level2_old.shape[0]
    group_index = level2_ids - narrow_index * group_size
    group_table = lax.broadcasted_iota(jnp.int32, (group_size, 1), 0) == group_index[None, :]
    group_sums = jnp.dot(group_table.astype(jnp.bfloat16), level1_new, preferred_element_type=jnp.float32)
    group_counts = jnp.dot(
        group_table.astype(jnp.bfloat16),
        jnp.ones((group_index.shape[0], 128), jnp.bfloat16),
        preferred_element_type=jnp.float32,
    )[:, 0]
    level1_float = level1_new.astype(jnp.float32)
    squares = jnp.sum(level1_float * level1_float, axis=1)
    group_squares = jnp.sum(jnp.where(group_table, squares[None, :], 0.0), axis=1)

    part_size = group_size // wide_count
    z_count = 8
    x_count = wide_count // z_count
    x_rings = [[z + z_count * x for x in range(x_count)] for z in range(z_count)]
    z_rings = [[z + z_count * x for z in range(z_count)] for x in range(x_count)]
    squares_high, squares_low = split_float(group_squares, 2)
    counts_high, counts_low = split_whole(group_counts, 16.0)
    sent_two = pack_columns(group_sums, [squares_high, squares_low, counts_high, counts_low])
    sent_two = sent_two.reshape(x_count, z_count, part_size, -1).transpose(1, 0, 2, 3)
    got_z = lax.all_to_all(sent_two, "wide", 0, 0, axis_index_groups=z_rings, tiled=True)
    z_sums = jnp.sum(got_z[:, :, :, :feature_dim].astype(jnp.float32), axis=0)
    z_tail = jnp.sum(got_z[:, :, :, feature_dim : feature_dim + 4].astype(jnp.float32), axis=0)
    z_squares = z_tail[:, :, 0] + z_tail[:, :, 1]
    z_counts = 16.0 * z_tail[:, :, 2] + z_tail[:, :, 3]
    squares_high, squares_low = split_float(z_squares.reshape(-1), 2)
    counts_high, counts_low = split_whole(z_counts.reshape(-1), 16.0)
    sent_x = pack_columns(z_sums.reshape(x_count * part_size, -1), [squares_high, squares_low, counts_high, counts_low])
    sent_x = sent_x.reshape(x_count, part_size, -1)
    got_two = lax.all_to_all(sent_x, "wide", 0, 0, axis_index_groups=x_rings, tiled=True)
    sums_two = jnp.sum(got_two[:, :, :feature_dim].astype(jnp.float32), axis=0)
    tail_two = jnp.sum(got_two[:, :, feature_dim : feature_dim + 4].astype(jnp.float32), axis=0)
    squares_two = tail_two[:, 0] + tail_two[:, 1]
    counts_two = 16.0 * tail_two[:, 2] + tail_two[:, 3]
    old_two = lax.dynamic_slice_in_dim(level2_old, wide_index * part_size, part_size, axis=0)
    means_two = (4.0 * old_two.astype(jnp.float32) + sums_two) / (4.0 + counts_two)[:, None]
    inertia = (
        squares_two
        - 2.0 * jnp.sum(means_two * sums_two, axis=1)
        + counts_two * jnp.sum(means_two * means_two, axis=1)
    )

    inertia_pieces = split_float(inertia, 3)
    sent_three = pack_columns(means_two, inertia_pieces)
    sent_three = jnp.broadcast_to(sent_three[None], (z_count,) + sent_three.shape)
    got_z = lax.all_to_all(sent_three, "wide", 0, 0, axis_index_groups=z_rings, tiled=True)
    sent_x = jnp.broadcast_to(got_z[None], (x_count,) + got_z.shape)
    got_three = lax.all_to_all(sent_x, "wide", 0, 0, axis_index_groups=x_rings, tiled=True)
    got_three = got_three.reshape(wide_count, part_size, -1)
    level2_new = got_three[:, :, :feature_dim].reshape(group_size, feature_dim)
    tail_three = got_three[:, :, feature_dim : feature_dim + 3].astype(jnp.float32)
    inertia_all = ((tail_three[:, :, 0] + tail_three[:, :, 1]) + tail_three[:, :, 2]).reshape(group_size)
    inertia_sum = lax.psum(jnp.sum(inertia_all), "narrow")
    centroid_total = float(group_size * narrow_count)
    split_weights = centroid_total * inertia_all / inertia_sum
    return (level1_new, level2_new, split_weights)


def solution(mesh):
    return jax.shard_map(
        local,
        mesh=mesh,
        in_specs=(
            P(("wide", "narrow"), None),
            P(("wide", "narrow")),
            P(("wide", "narrow")),
            P("wide", None),
            P("narrow", None),
            P("wide"),
        ),
        out_specs=(P("wide", None), P("narrow", None), P("narrow")),
        check_vma=False,
    )
```

```python
import jax
import jax.numpy as jnp
from jax import lax
from jax.sharding import PartitionSpec as P


def split_whole(values, step):
    high = jnp.floor(values / step)
    return high, values - step * high


def split_float(values, pieces):
    out = []
    rest = values
    for _ in range(pieces):
        piece = rest.astype(jnp.bfloat16)
        out.append(piece)
        rest = rest - piece.astype(jnp.float32)
    return out


def pack_columns(body, extras):
    rows = body.shape[0]
    lane = lax.broadcasted_iota(jnp.int32, (rows, 128), 1)
    tail = jnp.zeros((rows, 128), jnp.float32)
    for place, extra in enumerate(extras):
        tail = jnp.where(lane == place, extra.astype(jnp.float32)[:, None], tail)
    return jnp.concatenate([body.astype(jnp.bfloat16), tail.astype(jnp.bfloat16)], axis=1)


def local(embeddings, level1_ids, block_counts, level1_old, level2_old, level2_ids):
    wide_count = lax.axis_size("wide")
    narrow_count = lax.axis_size("narrow")
    wide_index = lax.axis_index("wide")
    narrow_index = lax.axis_index("narrow")
    slot_count = embeddings.shape[0] // wide_count
    feature_dim = embeddings.shape[1]
    owner_size = level1_old.shape[0]
    owner_base = wide_index * owner_size
    block_rows = embeddings.reshape(wide_count, slot_count, feature_dim)
    position = lax.broadcasted_iota(jnp.int32, (wide_count, slot_count), 1)
    live_slots = position < block_counts[:, None]
    sent_ids = jnp.where(live_slots, level1_ids.reshape(wide_count, slot_count), -1)
    got_rows = lax.all_to_all(block_rows, "wide", split_axis=0, concat_axis=0, tiled=True)
    got_ids = lax.all_to_all(sent_ids, "wide", split_axis=0, concat_axis=0, tiled=True)

    owner_index = got_ids.reshape(-1) - owner_base
    owner_table = lax.broadcasted_iota(jnp.int32, (owner_size, 1), 0) == owner_index[None, :]
    row_sums = jnp.dot(
        owner_table.astype(jnp.bfloat16),
        got_rows.reshape(-1, feature_dim),
        preferred_element_type=jnp.float32,
    )
    row_counts = jnp.dot(
        owner_table.astype(jnp.bfloat16),
        jnp.ones((owner_index.shape[0], 128), jnp.bfloat16),
        preferred_element_type=jnp.float32,
    )[:, 0]

    core_count = 2
    chip_count = narrow_count // core_count
    core = narrow_index % core_count
    chip = narrow_index // core_count
    half_size = owner_size // core_count
    sub_size = half_size // chip_count
    count_high, count_low = split_whole(row_counts, 16.0)
    packed = pack_columns(row_sums, [count_high, count_low]).reshape(core_count, half_size, -1)
    kept = jnp.where(core == 0, packed[0], packed[1])
    given = jnp.where(core == 0, packed[1], packed[0])
    partner = [(i, i ^ 1) for i in range(narrow_count)]
    chip_part = kept.astype(jnp.float32) + lax.ppermute(given, "narrow", partner).astype(jnp.float32)
    rings = [[c + core_count * y for y in range(chip_count)] for c in range(core_count)]
    sent_one = chip_part.astype(jnp.bfloat16).reshape(chip_count, sub_size, -1)
    got_one = lax.all_to_all(sent_one, "narrow", 0, 0, axis_index_groups=rings, tiled=True)
    sub_sums = jnp.sum(got_one[:, :, :feature_dim].astype(jnp.float32), axis=0)
    tail_sum = jnp.sum(got_one[:, :, feature_dim : feature_dim + 2].astype(jnp.float32), axis=0)
    sub_counts = 16.0 * tail_sum[:, 0] + tail_sum[:, 1]
    sub_start = core * half_size + chip * sub_size
    sub_old = lax.dynamic_slice_in_dim(level1_old, sub_start, sub_size, axis=0)
    sub_new = ((4.0 * sub_old.astype(jnp.float32) + sub_sums) / (4.0 + sub_counts)[:, None]).astype(jnp.bfloat16)
    sent_sub = jnp.broadcast_to(sub_new[None], (chip_count,) + sub_new.shape)
    half_new = lax.all_to_all(sent_sub, "narrow", 0, 0, axis_index_groups=rings, tiled=True).reshape(half_size, feature_dim)
    other_half = lax.ppermute(half_new, "narrow", partner)
    level1_new = jnp.where(
        core == 0,
        jnp.concatenate([half_new, other_half], axis=0),
        jnp.concatenate([other_half, half_new], axis=0),
    )

    group_size = level2_old.shape[0]
    group_index = level2_ids - narrow_index * group_size
    group_table = lax.broadcasted_iota(jnp.int32, (group_size, 1), 0) == group_index[None, :]
    group_sums = jnp.dot(group_table.astype(jnp.bfloat16), level1_new, preferred_element_type=jnp.float32)
    group_counts = jnp.dot(
        group_table.astype(jnp.bfloat16),
        jnp.ones((group_index.shape[0], 128), jnp.bfloat16),
        preferred_element_type=jnp.float32,
    )[:, 0]
    level1_float = level1_new.astype(jnp.float32)
    squares = jnp.sum(level1_float * level1_float, axis=1)
    group_squares = jnp.sum(jnp.where(group_table, squares[None, :], 0.0), axis=1)

    part_size = group_size // wide_count
    z_count = 8
    x_count = wide_count // z_count
    x_rings = [[z + z_count * x for x in range(x_count)] for z in range(z_count)]
    z_rings = [[z + z_count * x for z in range(z_count)] for x in range(x_count)]
    squares_high, squares_low = split_float(group_squares, 2)
    counts_high, counts_low = split_whole(group_counts, 16.0)
    sent_two = pack_columns(group_sums, [squares_high, squares_low, counts_high, counts_low])
    sent_two = sent_two.reshape(x_count, z_count * part_size, -1)
    got_x = lax.all_to_all(sent_two, "wide", 0, 0, axis_index_groups=x_rings, tiled=True)
    x_sums = jnp.sum(got_x[:, :, :feature_dim].astype(jnp.float32), axis=0)
    x_tail = jnp.sum(got_x[:, :, feature_dim : feature_dim + 4].astype(jnp.float32), axis=0)
    x_squares = x_tail[:, 0] + x_tail[:, 1]
    x_counts = 16.0 * x_tail[:, 2] + x_tail[:, 3]
    squares_high, squares_low = split_float(x_squares, 2)
    counts_high, counts_low = split_whole(x_counts, 16.0)
    sent_z = pack_columns(x_sums, [squares_high, squares_low, counts_high, counts_low])
    sent_z = sent_z.reshape(z_count, part_size, -1)
    got_two = lax.all_to_all(sent_z, "wide", 0, 0, axis_index_groups=z_rings, tiled=True)
    sums_two = jnp.sum(got_two[:, :, :feature_dim].astype(jnp.float32), axis=0)
    tail_two = jnp.sum(got_two[:, :, feature_dim : feature_dim + 4].astype(jnp.float32), axis=0)
    squares_two = tail_two[:, 0] + tail_two[:, 1]
    counts_two = 16.0 * tail_two[:, 2] + tail_two[:, 3]
    old_two = lax.dynamic_slice_in_dim(level2_old, wide_index * part_size, part_size, axis=0)
    means_two = (4.0 * old_two.astype(jnp.float32) + sums_two) / (4.0 + counts_two)[:, None]
    inertia = (
        squares_two
        - 2.0 * jnp.sum(means_two * sums_two, axis=1)
        + counts_two * jnp.sum(means_two * means_two, axis=1)
    )

    inertia_pieces = split_float(inertia, 3)
    sent_three = pack_columns(means_two, inertia_pieces)
    sent_three = jnp.broadcast_to(sent_three[None], (z_count,) + sent_three.shape)
    got_z = lax.all_to_all(sent_three, "wide", 0, 0, axis_index_groups=z_rings, tiled=True)
    sent_x = jnp.broadcast_to(got_z[None], (x_count,) + got_z.shape)
    got_three = lax.all_to_all(sent_x, "wide", 0, 0, axis_index_groups=x_rings, tiled=True)
    got_three = got_three.reshape(wide_count, part_size, -1)
    level2_new = got_three[:, :, :feature_dim].reshape(group_size, feature_dim)
    tail_three = got_three[:, :, feature_dim : feature_dim + 3].astype(jnp.float32)
    inertia_all = ((tail_three[:, :, 0] + tail_three[:, :, 1]) + tail_three[:, :, 2]).reshape(group_size)
    inertia_part = jnp.sum(inertia_all)
    inertia_chip = inertia_part + lax.ppermute(inertia_part, "narrow", partner)
    inertia_sum = lax.psum(inertia_chip, "narrow", axis_index_groups=rings)
    centroid_total = float(group_size * narrow_count)
    split_weights = centroid_total * inertia_all / inertia_sum
    return (level1_new, level2_new, split_weights)


def solution(mesh):
    return jax.shard_map(
        local,
        mesh=mesh,
        in_specs=(
            P(("wide", "narrow"), None),
            P(("wide", "narrow")),
            P(("wide", "narrow")),
            P("wide", None),
            P("narrow", None),
            P("wide"),
        ),
        out_specs=(P("wide", None), P("narrow", None), P("narrow")),
        check_vma=False,
    )
```

```python
import jax
import jax.numpy as jnp
from jax import lax
from jax.sharding import PartitionSpec as P


def split_whole(values, step):
    high = jnp.floor(values / step)
    return high, values - step * high


def split_float(values, pieces):
    out = []
    rest = values
    for _ in range(pieces):
        piece = rest.astype(jnp.bfloat16)
        out.append(piece)
        rest = rest - piece.astype(jnp.float32)
    return out


def pack_columns(body, extras):
    rows = body.shape[0]
    lane = lax.broadcasted_iota(jnp.int32, (rows, 128), 1)
    tail = jnp.zeros((rows, 128), jnp.float32)
    for place, extra in enumerate(extras):
        tail = jnp.where(lane == place, extra.astype(jnp.float32)[:, None], tail)
    return jnp.concatenate([body.astype(jnp.bfloat16), tail.astype(jnp.bfloat16)], axis=1)


def local(embeddings, level1_ids, block_counts, level1_old, level2_old, level2_ids):
    wide_count = lax.axis_size("wide")
    narrow_count = lax.axis_size("narrow")
    wide_index = lax.axis_index("wide")
    narrow_index = lax.axis_index("narrow")
    slot_count = embeddings.shape[0] // wide_count
    feature_dim = embeddings.shape[1]
    owner_size = level1_old.shape[0]
    owner_base = wide_index * owner_size
    block_rows = embeddings.reshape(wide_count, slot_count, feature_dim)
    position = lax.broadcasted_iota(jnp.int32, (wide_count, slot_count), 1)
    live_slots = position < block_counts[:, None]
    sent_ids = jnp.where(live_slots, level1_ids.reshape(wide_count, slot_count), -1)
    got_rows = lax.all_to_all(block_rows, "wide", split_axis=0, concat_axis=0, tiled=True)
    shifted = [jnp.take(sent_ids, wide_index, axis=0)]
    for shift in range(1, wide_count):
        chunk = jnp.take(sent_ids, (wide_index + shift) % wide_count, axis=0)
        pairs = [(i, (i + shift) % wide_count) for i in range(wide_count)]
        shifted.append(lax.ppermute(chunk, "wide", pairs))
    by_shift = jnp.stack(shifted)
    got_ids = jnp.take(by_shift, (wide_index - jnp.arange(wide_count)) % wide_count, axis=0)

    owner_index = got_ids.reshape(-1) - owner_base
    owner_table = lax.broadcasted_iota(jnp.int32, (owner_size, 1), 0) == owner_index[None, :]
    row_sums = jnp.dot(
        owner_table.astype(jnp.bfloat16),
        got_rows.reshape(-1, feature_dim),
        preferred_element_type=jnp.float32,
    )
    row_counts = jnp.dot(
        owner_table.astype(jnp.bfloat16),
        jnp.ones((owner_index.shape[0], 128), jnp.bfloat16),
        preferred_element_type=jnp.float32,
    )[:, 0]

    core_count = 2
    chip_count = narrow_count // core_count
    core = narrow_index % core_count
    chip = narrow_index // core_count
    half_size = owner_size // core_count
    sub_size = half_size // chip_count
    count_high, count_low = split_whole(row_counts, 16.0)
    packed = pack_columns(row_sums, [count_high, count_low]).reshape(core_count, half_size, -1)
    kept = jnp.where(core == 0, packed[0], packed[1])
    given = jnp.where(core == 0, packed[1], packed[0])
    partner = [(i, i ^ 1) for i in range(narrow_count)]
    chip_part = kept.astype(jnp.float32) + lax.ppermute(given, "narrow", partner).astype(jnp.float32)
    rings = [[c + core_count * y for y in range(chip_count)] for c in range(core_count)]
    sent_one = chip_part.astype(jnp.bfloat16).reshape(chip_count, sub_size, -1)
    got_one = lax.all_to_all(sent_one, "narrow", 0, 0, axis_index_groups=rings, tiled=True)
    sub_sums = jnp.sum(got_one[:, :, :feature_dim].astype(jnp.float32), axis=0)
    tail_sum = jnp.sum(got_one[:, :, feature_dim : feature_dim + 2].astype(jnp.float32), axis=0)
    sub_counts = 16.0 * tail_sum[:, 0] + tail_sum[:, 1]
    sub_start = core * half_size + chip * sub_size
    sub_old = lax.dynamic_slice_in_dim(level1_old, sub_start, sub_size, axis=0)
    sub_new = ((4.0 * sub_old.astype(jnp.float32) + sub_sums) / (4.0 + sub_counts)[:, None]).astype(jnp.bfloat16)
    sent_sub = jnp.broadcast_to(sub_new[None], (chip_count,) + sub_new.shape)
    half_new = lax.all_to_all(sent_sub, "narrow", 0, 0, axis_index_groups=rings, tiled=True).reshape(half_size, feature_dim)
    other_half = lax.ppermute(half_new, "narrow", partner)
    level1_new = jnp.where(
        core == 0,
        jnp.concatenate([half_new, other_half], axis=0),
        jnp.concatenate([other_half, half_new], axis=0),
    )

    group_size = level2_old.shape[0]
    group_index = level2_ids - narrow_index * group_size
    group_table = lax.broadcasted_iota(jnp.int32, (group_size, 1), 0) == group_index[None, :]
    group_sums = jnp.dot(group_table.astype(jnp.bfloat16), level1_new, preferred_element_type=jnp.float32)
    group_counts = jnp.dot(
        group_table.astype(jnp.bfloat16),
        jnp.ones((group_index.shape[0], 128), jnp.bfloat16),
        preferred_element_type=jnp.float32,
    )[:, 0]
    level1_float = level1_new.astype(jnp.float32)
    squares = jnp.sum(level1_float * level1_float, axis=1)
    group_squares = jnp.sum(jnp.where(group_table, squares[None, :], 0.0), axis=1)

    part_size = group_size // wide_count
    z_count = 8
    x_count = wide_count // z_count
    x_rings = [[z + z_count * x for x in range(x_count)] for z in range(z_count)]
    z_rings = [[z + z_count * x for z in range(z_count)] for x in range(x_count)]
    squares_high, squares_low = split_float(group_squares, 2)
    counts_high, counts_low = split_whole(group_counts, 16.0)
    sent_two = pack_columns(group_sums, [squares_high, squares_low, counts_high, counts_low])
    sent_two = sent_two.reshape(x_count, z_count * part_size, -1)
    got_x = lax.all_to_all(sent_two, "wide", 0, 0, axis_index_groups=x_rings, tiled=True)
    x_sums = jnp.sum(got_x[:, :, :feature_dim].astype(jnp.float32), axis=0)
    x_tail = jnp.sum(got_x[:, :, feature_dim : feature_dim + 4].astype(jnp.float32), axis=0)
    x_squares = x_tail[:, 0] + x_tail[:, 1]
    x_counts = 16.0 * x_tail[:, 2] + x_tail[:, 3]
    squares_high, squares_low = split_float(x_squares, 2)
    counts_high, counts_low = split_whole(x_counts, 16.0)
    sent_z = pack_columns(x_sums, [squares_high, squares_low, counts_high, counts_low])
    sent_z = sent_z.reshape(z_count, part_size, -1)
    got_two = lax.all_to_all(sent_z, "wide", 0, 0, axis_index_groups=z_rings, tiled=True)
    sums_two = jnp.sum(got_two[:, :, :feature_dim].astype(jnp.float32), axis=0)
    tail_two = jnp.sum(got_two[:, :, feature_dim : feature_dim + 4].astype(jnp.float32), axis=0)
    squares_two = tail_two[:, 0] + tail_two[:, 1]
    counts_two = 16.0 * tail_two[:, 2] + tail_two[:, 3]
    old_two = lax.dynamic_slice_in_dim(level2_old, wide_index * part_size, part_size, axis=0)
    means_two = (4.0 * old_two.astype(jnp.float32) + sums_two) / (4.0 + counts_two)[:, None]
    inertia = (
        squares_two
        - 2.0 * jnp.sum(means_two * sums_two, axis=1)
        + counts_two * jnp.sum(means_two * means_two, axis=1)
    )

    inertia_pieces = split_float(inertia, 3)
    sent_three = pack_columns(means_two, inertia_pieces)
    sent_three = jnp.broadcast_to(sent_three[None], (z_count,) + sent_three.shape)
    got_z = lax.all_to_all(sent_three, "wide", 0, 0, axis_index_groups=z_rings, tiled=True)
    sent_x = jnp.broadcast_to(got_z[None], (x_count,) + got_z.shape)
    got_three = lax.all_to_all(sent_x, "wide", 0, 0, axis_index_groups=x_rings, tiled=True)
    got_three = got_three.reshape(wide_count, part_size, -1)
    level2_new = got_three[:, :, :feature_dim].reshape(group_size, feature_dim)
    tail_three = got_three[:, :, feature_dim : feature_dim + 3].astype(jnp.float32)
    inertia_all = ((tail_three[:, :, 0] + tail_three[:, :, 1]) + tail_three[:, :, 2]).reshape(group_size)
    inertia_part = jnp.sum(inertia_all)
    inertia_chip = inertia_part + lax.ppermute(inertia_part, "narrow", partner)
    inertia_sum = lax.psum(inertia_chip, "narrow", axis_index_groups=rings)
    centroid_total = float(group_size * narrow_count)
    split_weights = centroid_total * inertia_all / inertia_sum
    return (level1_new, level2_new, split_weights)


def solution(mesh):
    return jax.shard_map(
        local,
        mesh=mesh,
        in_specs=(
            P(("wide", "narrow"), None),
            P(("wide", "narrow")),
            P(("wide", "narrow")),
            P("wide", None),
            P("narrow", None),
            P("wide"),
        ),
        out_specs=(P("wide", None), P("narrow", None), P("narrow")),
        check_vma=False,
    )
```

```python
import jax
import jax.numpy as jnp
from jax import lax
from jax.sharding import PartitionSpec as P


def split_whole(values, step):
    high = jnp.floor(values / step)
    return high, values - step * high


def split_float(values, pieces):
    out = []
    rest = values
    for _ in range(pieces):
        piece = rest.astype(jnp.bfloat16)
        out.append(piece)
        rest = rest - piece.astype(jnp.float32)
    return out


def pack_columns(body, extras):
    rows = body.shape[0]
    lane = lax.broadcasted_iota(jnp.int32, (rows, 128), 1)
    tail = jnp.zeros((rows, 128), jnp.float32)
    for place, extra in enumerate(extras):
        tail = jnp.where(lane == place, extra.astype(jnp.float32)[:, None], tail)
    return jnp.concatenate([body.astype(jnp.bfloat16), tail.astype(jnp.bfloat16)], axis=1)


def local(embeddings, level1_ids, block_counts, level1_old, level2_old, level2_ids):
    wide_count = lax.axis_size("wide")
    narrow_count = lax.axis_size("narrow")
    wide_index = lax.axis_index("wide")
    narrow_index = lax.axis_index("narrow")
    slot_count = embeddings.shape[0] // wide_count
    feature_dim = embeddings.shape[1]
    owner_size = level1_old.shape[0]
    owner_base = wide_index * owner_size
    block_rows = embeddings.reshape(wide_count, slot_count, feature_dim)
    position = lax.broadcasted_iota(jnp.int32, (wide_count, slot_count), 1)
    live_slots = position < block_counts[:, None]
    sent_ids = jnp.where(live_slots, level1_ids.reshape(wide_count, slot_count), -1)
    got_rows = lax.all_to_all(block_rows, "wide", split_axis=0, concat_axis=0, tiled=True)
    got_ids = lax.all_to_all(sent_ids, "wide", split_axis=0, concat_axis=0, tiled=True)

    owner_index = got_ids.reshape(-1) - owner_base
    core_count = 2
    chip_count = narrow_count // core_count
    core = narrow_index % core_count
    chip = narrow_index // core_count
    half_size = owner_size // core_count
    sub_size = half_size // chip_count
    rows_here = got_rows.reshape(-1, feature_dim)
    ones_here = jnp.ones((owner_index.shape[0], 128), jnp.bfloat16)

    def half_packed(half):
        half_ids = lax.broadcasted_iota(jnp.int32, (half_size, 1), 0) + half * half_size
        table = (half_ids == owner_index[None, :]).astype(jnp.bfloat16)
        sums = jnp.dot(table, rows_here, preferred_element_type=jnp.float32)
        counts = jnp.dot(table, ones_here, preferred_element_type=jnp.float32)[:, 0]
        count_high, count_low = split_whole(counts, 16.0)
        return pack_columns(sums, [count_high, count_low])

    partner = [(i, i ^ 1) for i in range(narrow_count)]
    given_back = lax.ppermute(half_packed(1 - core), "narrow", partner)
    chip_part = half_packed(core).astype(jnp.float32) + given_back.astype(jnp.float32)
    rings = [[c + core_count * y for y in range(chip_count)] for c in range(core_count)]
    sent_one = chip_part.astype(jnp.bfloat16).reshape(chip_count, sub_size, -1)
    got_one = lax.all_to_all(sent_one, "narrow", 0, 0, axis_index_groups=rings, tiled=True)
    sub_sums = jnp.sum(got_one[:, :, :feature_dim].astype(jnp.float32), axis=0)
    tail_sum = jnp.sum(got_one[:, :, feature_dim : feature_dim + 2].astype(jnp.float32), axis=0)
    sub_counts = 16.0 * tail_sum[:, 0] + tail_sum[:, 1]
    sub_start = core * half_size + chip * sub_size
    sub_old = lax.dynamic_slice_in_dim(level1_old, sub_start, sub_size, axis=0)
    sub_new = ((4.0 * sub_old.astype(jnp.float32) + sub_sums) / (4.0 + sub_counts)[:, None]).astype(jnp.bfloat16)
    sent_sub = jnp.broadcast_to(sub_new[None], (chip_count,) + sub_new.shape)
    half_new = lax.all_to_all(sent_sub, "narrow", 0, 0, axis_index_groups=rings, tiled=True).reshape(half_size, feature_dim)
    other_half = lax.ppermute(half_new, "narrow", partner)
    level1_new = jnp.where(
        core == 0,
        jnp.concatenate([half_new, other_half], axis=0),
        jnp.concatenate([other_half, half_new], axis=0),
    )

    group_size = level2_old.shape[0]
    group_index = level2_ids - narrow_index * group_size
    group_table = lax.broadcasted_iota(jnp.int32, (group_size, 1), 0) == group_index[None, :]
    group_sums = jnp.dot(group_table.astype(jnp.bfloat16), level1_new, preferred_element_type=jnp.float32)
    group_counts = jnp.dot(
        group_table.astype(jnp.bfloat16),
        jnp.ones((group_index.shape[0], 128), jnp.bfloat16),
        preferred_element_type=jnp.float32,
    )[:, 0]
    level1_float = level1_new.astype(jnp.float32)
    squares = jnp.sum(level1_float * level1_float, axis=1)
    group_squares = jnp.sum(jnp.where(group_table, squares[None, :], 0.0), axis=1)

    part_size = group_size // wide_count
    z_count = 8
    x_count = wide_count // z_count
    x_rings = [[z + z_count * x for x in range(x_count)] for z in range(z_count)]
    z_rings = [[z + z_count * x for z in range(z_count)] for x in range(x_count)]
    squares_high, squares_low = split_float(group_squares, 2)
    counts_high, counts_low = split_whole(group_counts, 16.0)
    sent_two = pack_columns(group_sums, [squares_high, squares_low, counts_high, counts_low])
    sent_two = sent_two.reshape(x_count, z_count * part_size, -1)
    got_x = lax.all_to_all(sent_two, "wide", 0, 0, axis_index_groups=x_rings, tiled=True)
    x_sums = jnp.sum(got_x[:, :, :feature_dim].astype(jnp.float32), axis=0)
    x_tail = jnp.sum(got_x[:, :, feature_dim : feature_dim + 4].astype(jnp.float32), axis=0)
    x_squares = x_tail[:, 0] + x_tail[:, 1]
    x_counts = 16.0 * x_tail[:, 2] + x_tail[:, 3]
    squares_high, squares_low = split_float(x_squares, 2)
    counts_high, counts_low = split_whole(x_counts, 16.0)
    sent_z = pack_columns(x_sums, [squares_high, squares_low, counts_high, counts_low])
    sent_z = sent_z.reshape(z_count, part_size, -1)
    got_two = lax.all_to_all(sent_z, "wide", 0, 0, axis_index_groups=z_rings, tiled=True)
    sums_two = jnp.sum(got_two[:, :, :feature_dim].astype(jnp.float32), axis=0)
    tail_two = jnp.sum(got_two[:, :, feature_dim : feature_dim + 4].astype(jnp.float32), axis=0)
    squares_two = tail_two[:, 0] + tail_two[:, 1]
    counts_two = 16.0 * tail_two[:, 2] + tail_two[:, 3]
    old_two = lax.dynamic_slice_in_dim(level2_old, wide_index * part_size, part_size, axis=0)
    means_two = (4.0 * old_two.astype(jnp.float32) + sums_two) / (4.0 + counts_two)[:, None]
    inertia = (
        squares_two
        - 2.0 * jnp.sum(means_two * sums_two, axis=1)
        + counts_two * jnp.sum(means_two * means_two, axis=1)
    )

    inertia_pieces = split_float(inertia, 3)
    sent_three = pack_columns(means_two, inertia_pieces)
    sent_three = jnp.broadcast_to(sent_three[None], (z_count,) + sent_three.shape)
    got_z = lax.all_to_all(sent_three, "wide", 0, 0, axis_index_groups=z_rings, tiled=True)
    sent_x = jnp.broadcast_to(got_z[None], (x_count,) + got_z.shape)
    got_three = lax.all_to_all(sent_x, "wide", 0, 0, axis_index_groups=x_rings, tiled=True)
    got_three = got_three.reshape(wide_count, part_size, -1)
    level2_new = got_three[:, :, :feature_dim].reshape(group_size, feature_dim)
    tail_three = got_three[:, :, feature_dim : feature_dim + 3].astype(jnp.float32)
    inertia_all = ((tail_three[:, :, 0] + tail_three[:, :, 1]) + tail_three[:, :, 2]).reshape(group_size)
    inertia_part = jnp.sum(inertia_all)
    inertia_chip = inertia_part + lax.ppermute(inertia_part, "narrow", partner)
    inertia_sum = lax.psum(inertia_chip, "narrow", axis_index_groups=rings)
    centroid_total = float(group_size * narrow_count)
    split_weights = centroid_total * inertia_all / inertia_sum
    return (level1_new, level2_new, split_weights)


def solution(mesh):
    return jax.shard_map(
        local,
        mesh=mesh,
        in_specs=(
            P(("wide", "narrow"), None),
            P(("wide", "narrow")),
            P(("wide", "narrow")),
            P("wide", None),
            P("narrow", None),
            P("wide"),
        ),
        out_specs=(P("wide", None), P("narrow", None), P("narrow")),
        check_vma=False,
    )
```

```python
import jax
import jax.numpy as jnp
from jax import lax
from jax.sharding import PartitionSpec as P


def split_whole(values, step):
    high = jnp.floor(values / step)
    return high, values - step * high


def split_float(values, pieces):
    out = []
    rest = values
    for _ in range(pieces):
        piece = rest.astype(jnp.bfloat16)
        out.append(piece)
        rest = rest - piece.astype(jnp.float32)
    return out


def pack_columns(body, extras):
    rows = body.shape[0]
    lane = lax.broadcasted_iota(jnp.int32, (rows, 128), 1)
    tail = jnp.zeros((rows, 128), jnp.float32)
    for place, extra in enumerate(extras):
        tail = jnp.where(lane == place, extra.astype(jnp.float32)[:, None], tail)
    return jnp.concatenate([body.astype(jnp.bfloat16), tail.astype(jnp.bfloat16)], axis=1)


def local(embeddings, level1_ids, block_counts, level1_old, level2_old, level2_ids):
    wide_count = lax.axis_size("wide")
    narrow_count = lax.axis_size("narrow")
    wide_index = lax.axis_index("wide")
    narrow_index = lax.axis_index("narrow")
    slot_count = embeddings.shape[0] // wide_count
    feature_dim = embeddings.shape[1]
    owner_size = level1_old.shape[0]
    owner_base = wide_index * owner_size
    block_rows = embeddings.reshape(wide_count, slot_count, feature_dim)
    position = lax.broadcasted_iota(jnp.int32, (wide_count, slot_count), 1)
    live_slots = position < block_counts[:, None]
    sent_ids = jnp.where(live_slots, level1_ids.reshape(wide_count, slot_count), -1)
    got_rows = lax.all_to_all(block_rows, "wide", split_axis=0, concat_axis=0, tiled=True)
    got_ids = lax.all_to_all(sent_ids, "wide", split_axis=0, concat_axis=0, tiled=True)

    owner_index = got_ids.reshape(-1) - owner_base
    core_count = 2
    chip_count = narrow_count // core_count
    core = narrow_index % core_count
    chip = narrow_index // core_count
    half_size = owner_size // core_count
    sub_size = half_size // chip_count
    rows_here = got_rows.reshape(-1, feature_dim)
    ones_here = jnp.ones((owner_index.shape[0], 128), jnp.bfloat16)

    def half_packed(half):
        half_ids = lax.broadcasted_iota(jnp.int32, (half_size, 1), 0) + half * half_size
        table = (half_ids == owner_index[None, :]).astype(jnp.bfloat16)
        sums = jnp.dot(table, rows_here, preferred_element_type=jnp.float32)
        counts = jnp.dot(table, ones_here, preferred_element_type=jnp.float32)[:, 0]
        count_high, count_low = split_whole(counts, 16.0)
        return pack_columns(sums, [count_high, count_low])

    partner = [(i, i ^ 1) for i in range(narrow_count)]
    given_back = lax.ppermute(half_packed(1 - core), "narrow", partner)
    chip_part = half_packed(core).astype(jnp.float32) + given_back.astype(jnp.float32)
    rings = [[c + core_count * y for y in range(chip_count)] for c in range(core_count)]
    sent_one = chip_part.astype(jnp.bfloat16).reshape(chip_count, sub_size, -1)
    got_one = lax.all_to_all(sent_one, "narrow", 0, 0, axis_index_groups=rings, tiled=True)
    sub_sums = jnp.sum(got_one[:, :, :feature_dim].astype(jnp.float32), axis=0)
    tail_sum = jnp.sum(got_one[:, :, feature_dim : feature_dim + 2].astype(jnp.float32), axis=0)
    sub_counts = 16.0 * tail_sum[:, 0] + tail_sum[:, 1]
    sub_start = core * half_size + chip * sub_size
    sub_old = lax.dynamic_slice_in_dim(level1_old, sub_start, sub_size, axis=0)
    sub_new = ((4.0 * sub_old.astype(jnp.float32) + sub_sums) / (4.0 + sub_counts)[:, None]).astype(jnp.bfloat16)
    sent_sub = jnp.broadcast_to(sub_new[None], (chip_count,) + sub_new.shape)
    half_new = lax.all_to_all(sent_sub, "narrow", 0, 0, axis_index_groups=rings, tiled=True).reshape(half_size, feature_dim)
    other_half = lax.ppermute(half_new, "narrow", partner)
    level1_new = jnp.where(
        core == 0,
        jnp.concatenate([half_new, other_half], axis=0),
        jnp.concatenate([other_half, half_new], axis=0),
    )

    group_size = level2_old.shape[0]
    group_index = level2_ids - narrow_index * group_size
    ones_half = jnp.ones((half_size, 128), jnp.bfloat16)

    def half_stats(half, rows):
        half_index = lax.dynamic_slice_in_dim(group_index, half * half_size, half_size)
        table = lax.broadcasted_iota(jnp.int32, (group_size, 1), 0) == half_index[None, :]
        sums = jnp.dot(table.astype(jnp.bfloat16), rows, preferred_element_type=jnp.float32)
        counts = jnp.dot(table.astype(jnp.bfloat16), ones_half, preferred_element_type=jnp.float32)[:, 0]
        rows_float = rows.astype(jnp.float32)
        squares = jnp.sum(rows_float * rows_float, axis=1)
        return sums, counts, jnp.sum(jnp.where(table, squares[None, :], 0.0), axis=1)

    own_stats = half_stats(core, half_new)
    other_stats = half_stats(1 - core, other_half)
    group_sums, group_counts, group_squares = (a + b for a, b in zip(own_stats, other_stats))

    part_size = group_size // wide_count
    z_count = 8
    x_count = wide_count // z_count
    x_rings = [[z + z_count * x for x in range(x_count)] for z in range(z_count)]
    z_rings = [[z + z_count * x for z in range(z_count)] for x in range(x_count)]
    squares_high, squares_low = split_float(group_squares, 2)
    counts_high, counts_low = split_whole(group_counts, 16.0)
    sent_two = pack_columns(group_sums, [squares_high, squares_low, counts_high, counts_low])
    sent_two = sent_two.reshape(x_count, z_count * part_size, -1)
    got_x = lax.all_to_all(sent_two, "wide", 0, 0, axis_index_groups=x_rings, tiled=True)
    x_sums = jnp.sum(got_x[:, :, :feature_dim].astype(jnp.float32), axis=0)
    x_tail = jnp.sum(got_x[:, :, feature_dim : feature_dim + 4].astype(jnp.float32), axis=0)
    x_squares = x_tail[:, 0] + x_tail[:, 1]
    x_counts = 16.0 * x_tail[:, 2] + x_tail[:, 3]
    squares_high, squares_low = split_float(x_squares, 2)
    counts_high, counts_low = split_whole(x_counts, 16.0)
    sent_z = pack_columns(x_sums, [squares_high, squares_low, counts_high, counts_low])
    sent_z = sent_z.reshape(z_count, part_size, -1)
    got_two = lax.all_to_all(sent_z, "wide", 0, 0, axis_index_groups=z_rings, tiled=True)
    sums_two = jnp.sum(got_two[:, :, :feature_dim].astype(jnp.float32), axis=0)
    tail_two = jnp.sum(got_two[:, :, feature_dim : feature_dim + 4].astype(jnp.float32), axis=0)
    squares_two = tail_two[:, 0] + tail_two[:, 1]
    counts_two = 16.0 * tail_two[:, 2] + tail_two[:, 3]
    old_two = lax.dynamic_slice_in_dim(level2_old, wide_index * part_size, part_size, axis=0)
    means_two = (4.0 * old_two.astype(jnp.float32) + sums_two) / (4.0 + counts_two)[:, None]
    inertia = (
        squares_two
        - 2.0 * jnp.sum(means_two * sums_two, axis=1)
        + counts_two * jnp.sum(means_two * means_two, axis=1)
    )

    inertia_pieces = split_float(inertia, 3)
    sent_three = pack_columns(means_two, inertia_pieces)
    sent_three = jnp.broadcast_to(sent_three[None], (z_count,) + sent_three.shape)
    got_z = lax.all_to_all(sent_three, "wide", 0, 0, axis_index_groups=z_rings, tiled=True)
    sent_x = jnp.broadcast_to(got_z[None], (x_count,) + got_z.shape)
    got_three = lax.all_to_all(sent_x, "wide", 0, 0, axis_index_groups=x_rings, tiled=True)
    got_three = got_three.reshape(wide_count, part_size, -1)
    level2_new = got_three[:, :, :feature_dim].reshape(group_size, feature_dim)
    tail_three = got_three[:, :, feature_dim : feature_dim + 3].astype(jnp.float32)
    inertia_all = ((tail_three[:, :, 0] + tail_three[:, :, 1]) + tail_three[:, :, 2]).reshape(group_size)
    inertia_part = jnp.sum(inertia_all)
    inertia_chip = inertia_part + lax.ppermute(inertia_part, "narrow", partner)
    inertia_sum = lax.psum(inertia_chip, "narrow", axis_index_groups=rings)
    centroid_total = float(group_size * narrow_count)
    split_weights = centroid_total * inertia_all / inertia_sum
    return (level1_new, level2_new, split_weights)


def solution(mesh):
    return jax.shard_map(
        local,
        mesh=mesh,
        in_specs=(
            P(("wide", "narrow"), None),
            P(("wide", "narrow")),
            P(("wide", "narrow")),
            P("wide", None),
            P("narrow", None),
            P("wide"),
        ),
        out_specs=(P("wide", None), P("narrow", None), P("narrow")),
        check_vma=False,
    )
```

```python
import jax
import jax.numpy as jnp
from jax import lax
from jax.sharding import PartitionSpec as P


def split_whole(values, step):
    high = jnp.floor(values / step)
    return high, values - step * high


def split_float(values, pieces):
    out = []
    rest = values
    for _ in range(pieces):
        piece = rest.astype(jnp.bfloat16)
        out.append(piece)
        rest = rest - piece.astype(jnp.float32)
    return out


def pack_columns(body, extras):
    rows = body.shape[0]
    lane = lax.broadcasted_iota(jnp.int32, (rows, 128), 1)
    tail = jnp.zeros((rows, 128), jnp.float32)
    for place, extra in enumerate(extras):
        tail = jnp.where(lane == place, extra.astype(jnp.float32)[:, None], tail)
    return jnp.concatenate([body.astype(jnp.bfloat16), tail.astype(jnp.bfloat16)], axis=1)


def local(embeddings, level1_ids, block_counts, level1_old, level2_old, level2_ids):
    wide_count = lax.axis_size("wide")
    narrow_count = lax.axis_size("narrow")
    wide_index = lax.axis_index("wide")
    narrow_index = lax.axis_index("narrow")
    slot_count = embeddings.shape[0] // wide_count
    feature_dim = embeddings.shape[1]
    owner_size = level1_old.shape[0]
    owner_base = wide_index * owner_size
    block_rows = embeddings.reshape(wide_count, slot_count, feature_dim)
    position = lax.broadcasted_iota(jnp.int32, (wide_count, slot_count), 1)
    live_slots = position < block_counts[:, None]
    sent_ids = jnp.where(live_slots, level1_ids.reshape(wide_count, slot_count), -1)
    got_rows = lax.all_to_all(block_rows, "wide", split_axis=0, concat_axis=0, tiled=True)
    id_z = 8
    id_x = wide_count // id_z
    ids_x_rings = [[z + id_z * x for x in range(id_x)] for z in range(id_z)]
    ids_z_rings = [[z + id_z * x for z in range(id_z)] for x in range(id_x)]
    ids_by_x = lax.all_to_all(sent_ids.reshape(id_x, id_z, slot_count), "wide", 0, 0, axis_index_groups=ids_x_rings, tiled=True)
    ids_by_z = lax.all_to_all(ids_by_x.transpose(1, 0, 2), "wide", 0, 0, axis_index_groups=ids_z_rings, tiled=True)
    got_ids = ids_by_z.transpose(1, 0, 2).reshape(wide_count, slot_count)

    owner_index = got_ids.reshape(-1) - owner_base
    core_count = 2
    chip_count = narrow_count // core_count
    core = narrow_index % core_count
    chip = narrow_index // core_count
    half_size = owner_size // core_count
    sub_size = half_size // chip_count
    rows_here = got_rows.reshape(-1, feature_dim)
    ones_here = jnp.ones((owner_index.shape[0], 128), jnp.bfloat16)

    def half_packed(half):
        half_ids = lax.broadcasted_iota(jnp.int32, (half_size, 1), 0) + half * half_size
        table = (half_ids == owner_index[None, :]).astype(jnp.bfloat16)
        sums = jnp.dot(table, rows_here, preferred_element_type=jnp.float32)
        counts = jnp.dot(table, ones_here, preferred_element_type=jnp.float32)[:, 0]
        count_high, count_low = split_whole(counts, 16.0)
        return pack_columns(sums, [count_high, count_low])

    partner = [(i, i ^ 1) for i in range(narrow_count)]
    given_back = lax.ppermute(half_packed(1 - core), "narrow", partner)
    chip_part = half_packed(core).astype(jnp.float32) + given_back.astype(jnp.float32)
    rings = [[c + core_count * y for y in range(chip_count)] for c in range(core_count)]
    sent_one = chip_part.astype(jnp.bfloat16).reshape(chip_count, sub_size, -1)
    got_one = lax.all_to_all(sent_one, "narrow", 0, 0, axis_index_groups=rings, tiled=True)
    sub_sums = jnp.sum(got_one[:, :, :feature_dim].astype(jnp.float32), axis=0)
    tail_sum = jnp.sum(got_one[:, :, feature_dim : feature_dim + 2].astype(jnp.float32), axis=0)
    sub_counts = 16.0 * tail_sum[:, 0] + tail_sum[:, 1]
    sub_start = core * half_size + chip * sub_size
    sub_old = lax.dynamic_slice_in_dim(level1_old, sub_start, sub_size, axis=0)
    sub_new = ((4.0 * sub_old.astype(jnp.float32) + sub_sums) / (4.0 + sub_counts)[:, None]).astype(jnp.bfloat16)
    sent_sub = jnp.broadcast_to(sub_new[None], (chip_count,) + sub_new.shape)
    half_new = lax.all_to_all(sent_sub, "narrow", 0, 0, axis_index_groups=rings, tiled=True).reshape(half_size, feature_dim)
    other_half = lax.ppermute(half_new, "narrow", partner)
    level1_new = jnp.where(
        core == 0,
        jnp.concatenate([half_new, other_half], axis=0),
        jnp.concatenate([other_half, half_new], axis=0),
    )

    group_size = level2_old.shape[0]
    group_index = level2_ids - narrow_index * group_size
    group_table = lax.broadcasted_iota(jnp.int32, (group_size, 1), 0) == group_index[None, :]
    group_sums = jnp.dot(group_table.astype(jnp.bfloat16), level1_new, preferred_element_type=jnp.float32)
    group_counts = jnp.dot(
        group_table.astype(jnp.bfloat16),
        jnp.ones((group_index.shape[0], 128), jnp.bfloat16),
        preferred_element_type=jnp.float32,
    )[:, 0]
    level1_float = level1_new.astype(jnp.float32)
    squares = jnp.sum(level1_float * level1_float, axis=1)
    group_squares = jnp.sum(jnp.where(group_table, squares[None, :], 0.0), axis=1)

    part_size = group_size // wide_count
    z_count = 8
    x_count = wide_count // z_count
    x_rings = [[z + z_count * x for x in range(x_count)] for z in range(z_count)]
    z_rings = [[z + z_count * x for z in range(z_count)] for x in range(x_count)]
    squares_high, squares_low = split_float(group_squares, 2)
    counts_high, counts_low = split_whole(group_counts, 16.0)
    sent_two = pack_columns(group_sums, [squares_high, squares_low, counts_high, counts_low])
    sent_two = sent_two.reshape(x_count, z_count * part_size, -1)
    got_x = lax.all_to_all(sent_two, "wide", 0, 0, axis_index_groups=x_rings, tiled=True)
    x_sums = jnp.sum(got_x[:, :, :feature_dim].astype(jnp.float32), axis=0)
    x_tail = jnp.sum(got_x[:, :, feature_dim : feature_dim + 4].astype(jnp.float32), axis=0)
    x_squares = x_tail[:, 0] + x_tail[:, 1]
    x_counts = 16.0 * x_tail[:, 2] + x_tail[:, 3]
    squares_high, squares_low = split_float(x_squares, 2)
    counts_high, counts_low = split_whole(x_counts, 16.0)
    sent_z = pack_columns(x_sums, [squares_high, squares_low, counts_high, counts_low])
    sent_z = sent_z.reshape(z_count, part_size, -1)
    got_two = lax.all_to_all(sent_z, "wide", 0, 0, axis_index_groups=z_rings, tiled=True)
    sums_two = jnp.sum(got_two[:, :, :feature_dim].astype(jnp.float32), axis=0)
    tail_two = jnp.sum(got_two[:, :, feature_dim : feature_dim + 4].astype(jnp.float32), axis=0)
    squares_two = tail_two[:, 0] + tail_two[:, 1]
    counts_two = 16.0 * tail_two[:, 2] + tail_two[:, 3]
    old_two = lax.dynamic_slice_in_dim(level2_old, wide_index * part_size, part_size, axis=0)
    means_two = (4.0 * old_two.astype(jnp.float32) + sums_two) / (4.0 + counts_two)[:, None]
    inertia = (
        squares_two
        - 2.0 * jnp.sum(means_two * sums_two, axis=1)
        + counts_two * jnp.sum(means_two * means_two, axis=1)
    )

    inertia_pieces = split_float(inertia, 3)
    sent_three = pack_columns(means_two, inertia_pieces)
    sent_three = jnp.broadcast_to(sent_three[None], (z_count,) + sent_three.shape)
    got_z = lax.all_to_all(sent_three, "wide", 0, 0, axis_index_groups=z_rings, tiled=True)
    sent_x = jnp.broadcast_to(got_z[None], (x_count,) + got_z.shape)
    got_three = lax.all_to_all(sent_x, "wide", 0, 0, axis_index_groups=x_rings, tiled=True)
    got_three = got_three.reshape(wide_count, part_size, -1)
    level2_new = got_three[:, :, :feature_dim].reshape(group_size, feature_dim)
    tail_three = got_three[:, :, feature_dim : feature_dim + 3].astype(jnp.float32)
    inertia_all = ((tail_three[:, :, 0] + tail_three[:, :, 1]) + tail_three[:, :, 2]).reshape(group_size)
    inertia_part = jnp.sum(inertia_all)
    inertia_chip = inertia_part + lax.ppermute(inertia_part, "narrow", partner)
    inertia_sum = lax.psum(inertia_chip, "narrow", axis_index_groups=rings)
    centroid_total = float(group_size * narrow_count)
    split_weights = centroid_total * inertia_all / inertia_sum
    return (level1_new, level2_new, split_weights)


def solution(mesh):
    return jax.shard_map(
        local,
        mesh=mesh,
        in_specs=(
            P(("wide", "narrow"), None),
            P(("wide", "narrow")),
            P(("wide", "narrow")),
            P("wide", None),
            P("narrow", None),
            P("wide"),
        ),
        out_specs=(P("wide", None), P("narrow", None), P("narrow")),
        check_vma=False,
    )
```

```python
import jax
import jax.numpy as jnp
from jax import lax
from jax.sharding import PartitionSpec as P


def split_whole(values, step):
    high = jnp.floor(values / step)
    return high, values - step * high


def split_float(values, pieces):
    out = []
    rest = values
    for _ in range(pieces):
        piece = rest.astype(jnp.bfloat16)
        out.append(piece)
        rest = rest - piece.astype(jnp.float32)
    return out


def pack_columns(body, extras):
    rows = body.shape[0]
    lane = lax.broadcasted_iota(jnp.int32, (rows, 128), 1)
    tail = jnp.zeros((rows, 128), jnp.float32)
    for place, extra in enumerate(extras):
        tail = jnp.where(lane == place, extra.astype(jnp.float32)[:, None], tail)
    return jnp.concatenate([body.astype(jnp.bfloat16), tail.astype(jnp.bfloat16)], axis=1)


def local(embeddings, level1_ids, block_counts, level1_old, level2_old, level2_ids):
    wide_count = lax.axis_size("wide")
    narrow_count = lax.axis_size("narrow")
    wide_index = lax.axis_index("wide")
    narrow_index = lax.axis_index("narrow")
    slot_count = embeddings.shape[0] // wide_count
    feature_dim = embeddings.shape[1]
    owner_size = level1_old.shape[0]
    owner_base = wide_index * owner_size
    block_rows = embeddings.reshape(wide_count, slot_count, feature_dim)
    position = lax.broadcasted_iota(jnp.int32, (wide_count, slot_count), 1)
    live_slots = position < block_counts[:, None]
    sent_ids = jnp.where(live_slots, level1_ids.reshape(wide_count, slot_count), -1)
    got_rows = lax.all_to_all(block_rows, "wide", split_axis=0, concat_axis=0, tiled=True)
    got_ids = lax.all_to_all(sent_ids, "wide", split_axis=0, concat_axis=0, tiled=True)

    owner_index = got_ids.reshape(-1) - owner_base
    core_count = 2
    chip_count = narrow_count // core_count
    core = narrow_index % core_count
    chip = narrow_index // core_count
    half_size = owner_size // core_count
    sub_size = half_size // chip_count
    rows_here = got_rows.reshape(-1, feature_dim)
    ones_here = jnp.ones((owner_index.shape[0], 128), jnp.bfloat16)

    def half_packed(half):
        half_ids = lax.broadcasted_iota(jnp.int32, (half_size, 1), 0) + half * half_size
        table = (half_ids == owner_index[None, :]).astype(jnp.bfloat16)
        sums = jnp.dot(table, rows_here, preferred_element_type=jnp.float32)
        counts = jnp.dot(table, ones_here, preferred_element_type=jnp.float32)[:, 0]
        count_high, count_low = split_whole(counts, 16.0)
        return pack_columns(sums, [count_high, count_low])

    partner = [(i, i ^ 1) for i in range(narrow_count)]
    given_back = lax.ppermute(half_packed(1 - core), "narrow", partner)
    chip_part = half_packed(core).astype(jnp.float32) + given_back.astype(jnp.float32)
    rings = [[c + core_count * y for y in range(chip_count)] for c in range(core_count)]
    sent_one = chip_part.astype(jnp.bfloat16).reshape(chip_count, sub_size, -1)
    got_one = lax.all_to_all(sent_one, "narrow", 0, 0, axis_index_groups=rings, tiled=True)
    sub_sums = jnp.sum(got_one[:, :, :feature_dim].astype(jnp.float32), axis=0)
    tail_sum = jnp.sum(got_one[:, :, feature_dim : feature_dim + 2].astype(jnp.float32), axis=0)
    sub_counts = 16.0 * tail_sum[:, 0] + tail_sum[:, 1]
    sub_start = core * half_size + chip * sub_size
    sub_old = lax.dynamic_slice_in_dim(level1_old, sub_start, sub_size, axis=0)
    sub_new = ((4.0 * sub_old.astype(jnp.float32) + sub_sums) / (4.0 + sub_counts)[:, None]).astype(jnp.bfloat16)
    sent_sub = jnp.broadcast_to(sub_new[None], (chip_count,) + sub_new.shape)
    half_new = lax.all_to_all(sent_sub, "narrow", 0, 0, axis_index_groups=rings, tiled=True).reshape(half_size, feature_dim)
    other_half = lax.ppermute(half_new, "narrow", partner)
    level1_new = jnp.where(
        core == 0,
        jnp.concatenate([half_new, other_half], axis=0),
        jnp.concatenate([other_half, half_new], axis=0),
    )

    group_size = level2_old.shape[0]
    group_index = level2_ids - narrow_index * group_size
    group_table = lax.broadcasted_iota(jnp.int32, (group_size, 1), 0) == group_index[None, :]
    group_sums = jnp.dot(group_table.astype(jnp.bfloat16), level1_new, preferred_element_type=jnp.float32)
    group_counts = jnp.dot(
        group_table.astype(jnp.bfloat16),
        jnp.ones((group_index.shape[0], 128), jnp.bfloat16),
        preferred_element_type=jnp.float32,
    )[:, 0]
    level1_float = level1_new.astype(jnp.float32)
    squares = jnp.sum(level1_float * level1_float, axis=1)
    group_squares = jnp.sum(jnp.where(group_table, squares[None, :], 0.0), axis=1)

    part_size = group_size // wide_count
    z_count = 8
    x_count = wide_count // z_count
    x_rings = [[z + z_count * x for x in range(x_count)] for z in range(z_count)]
    z_rings = [[z + z_count * x for z in range(z_count)] for x in range(x_count)]
    squares_high, squares_low = split_float(group_squares, 2)
    counts_high, counts_low = split_whole(group_counts, 16.0)
    sent_two = pack_columns(group_sums, [squares_high, squares_low, counts_high, counts_low])
    sent_two = sent_two.reshape(x_count, z_count * part_size, -1)
    got_x = lax.all_to_all(sent_two, "wide", 0, 0, axis_index_groups=x_rings, tiled=True)
    x_sums = jnp.sum(got_x[:, :, :feature_dim].astype(jnp.float32), axis=0)
    x_tail = jnp.sum(got_x[:, :, feature_dim : feature_dim + 4].astype(jnp.float32), axis=0)
    x_squares = x_tail[:, 0] + x_tail[:, 1]
    x_counts = 16.0 * x_tail[:, 2] + x_tail[:, 3]
    squares_high, squares_low = split_float(x_squares, 2)
    counts_high, counts_low = split_whole(x_counts, 16.0)
    sent_z = pack_columns(x_sums, [squares_high, squares_low, counts_high, counts_low])
    sent_z = sent_z.reshape(z_count, part_size, -1)
    got_two = lax.all_to_all(sent_z, "wide", 0, 0, axis_index_groups=z_rings, tiled=True)
    sums_two = jnp.sum(got_two[:, :, :feature_dim].astype(jnp.float32), axis=0)
    tail_two = jnp.sum(got_two[:, :, feature_dim : feature_dim + 4].astype(jnp.float32), axis=0)
    squares_two = tail_two[:, 0] + tail_two[:, 1]
    counts_two = 16.0 * tail_two[:, 2] + tail_two[:, 3]
    old_two = lax.dynamic_slice_in_dim(level2_old, wide_index * part_size, part_size, axis=0)
    means_two = (4.0 * old_two.astype(jnp.float32) + sums_two) / (4.0 + counts_two)[:, None]
    inertia = (
        squares_two
        - 2.0 * jnp.sum(means_two * sums_two, axis=1)
        + counts_two * jnp.sum(means_two * means_two, axis=1)
    )

    inertia_pieces = split_float(inertia, 3)
    sent_three = pack_columns(means_two, inertia_pieces)
    sent_three = jnp.broadcast_to(sent_three[None], (z_count,) + sent_three.shape)
    got_z = lax.all_to_all(sent_three, "wide", 0, 0, axis_index_groups=z_rings, tiled=True)
    sent_x = jnp.broadcast_to(got_z[None], (x_count,) + got_z.shape)
    got_three = lax.all_to_all(sent_x, "wide", 0, 0, axis_index_groups=x_rings, tiled=True)
    got_three = got_three.reshape(wide_count, part_size, -1)
    level2_new = got_three[:, :, :feature_dim].reshape(group_size, feature_dim)
    tail_three = got_three[:, :, feature_dim : feature_dim + 3].astype(jnp.float32)
    inertia_all = ((tail_three[:, :, 0] + tail_three[:, :, 1]) + tail_three[:, :, 2]).reshape(group_size)
    inertia_part = jnp.sum(inertia_all)
    inertia_chip = inertia_part + lax.ppermute(inertia_part, "narrow", partner)
    inertia_sum = inertia_chip
    for step in range(1, chip_count.bit_length() - 1 + 1):
        mask = core_count << (step - 1)
        inertia_sum = inertia_sum + lax.ppermute(inertia_sum, "narrow", [(i, i ^ mask) for i in range(narrow_count)])
    centroid_total = float(group_size * narrow_count)
    split_weights = centroid_total * inertia_all / inertia_sum
    return (level1_new, level2_new, split_weights)


def solution(mesh):
    return jax.shard_map(
        local,
        mesh=mesh,
        in_specs=(
            P(("wide", "narrow"), None),
            P(("wide", "narrow")),
            P(("wide", "narrow")),
            P("wide", None),
            P("narrow", None),
            P("wide"),
        ),
        out_specs=(P("wide", None), P("narrow", None), P("narrow")),
        check_vma=False,
    )
```
